512 devices in a mesh: panel: 2 (over y_hi), gx: 16 (over x, y_lo), gy: 16 (over z, core).
Axes of the slice: x: 4, y: 8 (y_hi: 2, y_lo: 4; y = y_hi * 4 + y_lo), z: 8, core: 2. Of those that a mesh axis runs over, the one named last changes fastest.
Arguments:
- state: float32 [2, 3, 1, 2048, 2048], P('panel', None, None, 'gx', 'gy'), may hold values from -6 to 6
- coriolis: float32 [2, 2048, 2048], P('panel', 'gx', 'gy'), may hold values from -1.5 to 1.5
- edge_rotation: int32 [2, 4], P('panel'), may hold values from 0 to 3
- nest_block_state: float32 [2, 16, 256, 3, 1, 576], P('panel', 'gx', 'gy'), may hold values from -6 to 6
- parent_tile_index: int32 [2, 16, 256, 1], P('panel', 'gx', 'gy'), may hold values from 0 to 15; in each aligned block of 16 rows (0 to 15, 16 to 31, ..., all dimensions but the last counted through in order) at most 2 rows name the same one
- parent_spot_index: int32 [2, 16, 256], P('panel', 'gx', 'gy'), may hold values from 0 to 255
Outputs:
- parent_out: float32 [2, 3, 1, 2048, 2048], P('panel', None, None, 'gx', 'gy')
- nest_out: float32 [2, 16, 256, 3, 1, 576], P('panel', 'gx', 'gy')
The draws below stay inside these ranges and needn't reach their ends.
Inputs may be any that keep to these rules, and one draw needn't show every extreme that they name: `parent_tile_index`: among the 16 nest blocks that one device owns (aligned blocks of 16 along the line), no tile of the line is named more than 2 times, and in every draw some device names one tile exactly 2 times.
All inputs are finite; a program needn't handle non-finite values.
Results may differ from the reference program's by a relative error of at most 0.0003.
Values sent between devices are 32-bit elements; how exact they have to be, the bound alone decides.
No kernel may reach another device: no remote copies, remote signals or barrier semaphores. Data moves between devices by JAX's collectives and lax.ppermute only.
A program may use at most 64 MiB of HBM per device.

```python
import math
import jax
import jax.numpy as jnp
import numpy as np
from jax import lax

TILE = 128
LEVEL_COUNT = 1
OWNED_NEST = 16
NSUB = 2
PATCH = 8
RATIO = 3
LINE_TILES = 16
FIRST_DIM_LINES = 16
NX = 2048
NY = 2048
LINE_NEST_BLOCKS = 256
PARENT_CAPACITY = 2
QN = 16
BLOCK_SPOTS = 256
FINE = 24
NEST_CELLS2 = 576


def plant(array, stream_key, least, largest):
    shape = array.shape
    place = [jax.random.randint(jax.random.fold_in(stream_key, axis), (), 0, shape[axis]) for axis in range(len(shape))]
    array = array.at[tuple(place)].set(least)
    longest = shape.index(max(shape))
    place[longest] = (place[longest] + 1) % shape[longest]
    return array.at[tuple(place)].set(largest)


def block_scale(stream_key, dims, split, low, largest):
    loudness, own = 1.0, jax.random.fold_in(stream_key, 6)
    for axis_at, blocks in split:
        heights = jnp.exp(jax.random.uniform(jax.random.fold_in(own, axis_at), (blocks,), jnp.float32, low / len(split), largest / len(split)))
        loudness = loudness * jnp.repeat(heights, dims[axis_at] // blocks).reshape([-1 if axis == axis_at else 1 for axis in range(len(dims))])
    return loudness


def assign_block(rng, own, number, rows, amount, top, limit, lean):
    order = jax.random.permutation(rng, amount)
    heavy_load, usual = shares(amount, rows * top, limit, lean, True), shares(amount, rows * top, limit, lean, False)
    places = jnp.arange(amount)

    def named(tallies, offset_by):
        used = int((tallies > 0).sum())
        fixed = max(1, used // 4)
        moved = fixed + (places - fixed + offset_by * (used - fixed)) % max(1, amount - fixed)
        return jnp.zeros((amount,), jnp.int32).at[order[jnp.where(places < fixed, places, moved)]].set(jnp.asarray(tallies, jnp.int32))

    tallies = jnp.where(number % 4 == 0, named(heavy_load, number // 4), named(usual, number - number // 4 - 1))
    mixed = jax.random.permutation(jax.random.fold_in(own, 3), amount)
    giver, receiver = mixed[0:amount // 2 * 2:2], mixed[1:amount // 2 * 2:2]
    slack = jnp.minimum(tallies[giver] - 1, limit - tallies[receiver]) // 2
    slack = jnp.where((giver == order[0]) | (receiver == order[0]) | (tallies[receiver] == 0), 0, jnp.maximum(slack, 0))
    moved = jax.random.randint(jax.random.fold_in(own, 4), (amount // 2,), 0, 1 << 20) % (slack + 1)
    tallies = tallies.at[giver].add(-moved).at[receiver].add(moved)
    items = jnp.searchsorted(jnp.cumsum(tallies), jnp.arange(rows * top), side="right").astype(jnp.int32)
    listing = items.reshape(top, rows).T
    listing = listing[jax.random.permutation(jax.random.fold_in(own, 1), rows)]
    offset_by = jax.random.randint(jax.random.fold_in(own, 2), (rows, 1), 0, top)
    return jnp.take_along_axis(listing, (jnp.arange(top)[None, :] + offset_by) % top, axis=1)


def shares(amount, total, limit, slope, full):
    portions = [(1 << 20) // math.isqrt(standing ** slope) + 1 for standing in range(1, amount + 1)]
    largest = limit if full else min(limit, max(-(-total // amount), total * portions[0] // sum(portions)))
    least = 1 if total - largest >= amount - 1 else 0
    given, rest = [largest] + [least] * (amount - 1), total - largest - least * (amount - 1)
    while rest > 0:
        free = [i for i in range(1, amount) if given[i] < largest] or [i for i in range(1, amount) if given[i] < limit]
        mass, remaining = sum([portions[i] for i in free]), rest
        for i in free:
            addition = min(limit - given[i], max(1, remaining * portions[i] // mass), rest)
            given[i] = given[i] + addition
            rest = rest - addition
    return np.array(given)


def noise(rng, shape, deviation, reach, pieces=(), kind=jnp.bfloat16):
    values = deviation * jax.random.normal(rng, shape, jnp.float32)
    if pieces:
        values = values * block_scale(rng, shape, pieces, -0.22, 0.18)
    return jnp.clip(values, -reach, reach).astype(kind)


def setup_inputs(seed: int = 0) -> dict:
    key_of = jax.random.split(jax.random.key(seed), 7)
    state = noise(key_of[0], (2, 3, LEVEL_COUNT, NX, NY), 1.0, 6.0, ((0, 2), (3, 16), (4, 16)), jnp.float32)
    coriolis = jnp.clip(jax.random.uniform(key_of[1], (2, NX, NY), jnp.float32, -1.5, 1.5) * block_scale(key_of[1], (2, NX, NY), ((0, 2), (1, 16), (2, 16)), -0.4, 0.0), -1.5, 1.5)
    edge_rotation = plant(jax.random.randint(key_of[2], (2, 4), 0, 4), jax.random.fold_in(key_of[2], 1), 0, 3).astype(jnp.int32)
    nest_block_state = noise(key_of[3], (2, FIRST_DIM_LINES, LINE_NEST_BLOCKS, 3, LEVEL_COUNT, NEST_CELLS2), 1.0, 6.0, ((0, 2), (1, 16), (2, 16)), jnp.float32)
    parent_tile_index_keys = jax.random.split(jax.random.fold_in(key_of[4], 1), 2 * FIRST_DIM_LINES * LINE_NEST_BLOCKS // OWNED_NEST)
    parent_tile_index_turns = jax.random.permutation(jax.random.fold_in(key_of[4], 3), 2 * FIRST_DIM_LINES * LINE_NEST_BLOCKS // OWNED_NEST)
    parent_tile_index = jax.vmap(lambda own, number: assign_block(jax.random.fold_in(key_of[4], 2), own, number, OWNED_NEST, LINE_TILES, 1, PARENT_CAPACITY, 2))(parent_tile_index_keys, parent_tile_index_turns).reshape((2, FIRST_DIM_LINES, LINE_NEST_BLOCKS, 1))
    parent_spot_index = plant(jax.random.randint(key_of[5], (2, FIRST_DIM_LINES, LINE_NEST_BLOCKS), 0, BLOCK_SPOTS), jax.random.fold_in(key_of[5], 1), 0, BLOCK_SPOTS - 1).astype(jnp.int32)
    return dict(state=state, coriolis=coriolis, edge_rotation=edge_rotation, nest_block_state=nest_block_state, parent_tile_index=parent_tile_index, parent_spot_index=parent_spot_index)


DT_STEP = 0.25
GRAVITY = 1.0
DAMPING = 0.5
DEPTH = 1.0
KAPPA = 0.2
ALPHA = 0.5
BETA = 0.5


def rotated(code, east_part, north_part):
    along = (code == 0).astype(east_part.dtype) - (code == 2).astype(east_part.dtype)
    across = (code == 3).astype(east_part.dtype) - (code == 1).astype(east_part.dtype)
    return along * east_part + across * north_part, along * north_part - across * east_part


def centre(field):
    return field[..., 1:-1, 1:-1]


def along_x(field):
    return 0.5 * (field[..., 2:, 1:-1] - field[..., :-2, 1:-1])


def along_y(field):
    return 0.5 * (field[..., 1:-1, 2:] - field[..., 1:-1, :-2])


def laplacian(field):
    return field[..., 2:, 1:-1] + field[..., :-2, 1:-1] + field[..., 1:-1, 2:] + field[..., 1:-1, :-2] - 4.0 * centre(field)


def advance(height, east, north, coriolis):
    absolute = coriolis + along_x(north) - along_y(east)
    depth = DEPTH + height
    divergence = along_x(depth * east) + along_y(depth * north)
    new_height = centre(height) - DT_STEP * divergence
    new_east = centre(east) + DT_STEP * (absolute * centre(north) - GRAVITY * along_x(height) + DAMPING * laplacian(east))
    new_north = centre(north) + DT_STEP * (-absolute * centre(east) - GRAVITY * along_y(height) + DAMPING * laplacian(north))
    return new_height, new_east, new_north


def fill_cycle(level, codes):
    other = level[::-1]
    padded = jnp.pad(level, ((0, 0), (0, 0), (1, 1), (1, 1)))
    sides = [other[:, :, 0, :], other[:, :, -1, :], other[:, :, :, 0], other[:, :, :, -1]]
    for side in range(4):
        strip = sides[side]
        code = codes[:, side][:, None]
        east_rot, north_rot = rotated(code, strip[:, 1], strip[:, 2])
        strip = jnp.stack([strip[:, 0], east_rot, north_rot], axis=1)
        if side == 0:
            padded = padded.at[:, :, 0, 1:-1].set(strip)
        elif side == 1:
            padded = padded.at[:, :, -1, 1:-1].set(strip)
        elif side == 2:
            padded = padded.at[:, :, 1:-1, 0].set(strip)
        else:
            padded = padded.at[:, :, 1:-1, -1].set(strip)
    return padded


def smooth_blocks(blocks):
    count = blocks.shape[0]
    square = blocks.reshape(count, 3, blocks.shape[2], FINE, FINE)
    padded = jnp.pad(square, ((0, 0), (0, 0), (0, 0), (1, 1), (1, 1)), mode="edge")
    return (square + KAPPA * laplacian(padded)).reshape(blocks.shape)


def blend_nest(blocks, parent):
    count = blocks.shape[0]
    coarse = parent.reshape(count, 3, blocks.shape[2], PATCH, PATCH)
    upsampled = jnp.repeat(jnp.repeat(coarse, RATIO, axis=3), RATIO, axis=4).reshape(blocks.shape)
    smoothed = smooth_blocks(blocks)
    return smoothed + ALPHA * (upsampled - smoothed)


def block_means(blocks):
    count = blocks.shape[0]
    grouped = blocks.reshape(count, 3, blocks.shape[2], PATCH, RATIO, PATCH, RATIO)
    return jnp.mean(grouped, axis=(4, 6)).reshape(count, -1)


def line_rows(line):
    shaped = line.reshape(3, LEVEL_COUNT, QN, PATCH, LINE_TILES, QN, PATCH)
    return jnp.transpose(shaped, (4, 2, 5, 0, 1, 3, 6)).reshape(LINE_TILES * BLOCK_SPOTS, 3 * LEVEL_COUNT * PATCH * PATCH)


def line_field(rows):
    shaped = rows.reshape(LINE_TILES, QN, QN, 3, LEVEL_COUNT, PATCH, PATCH)
    return jnp.transpose(shaped, (3, 4, 1, 5, 0, 2, 6)).reshape(3, LEVEL_COUNT, TILE, NY)


def reference(state, coriolis, edge_rotation, nest_block_state, parent_tile_index, parent_spot_index):
    levels_first = jnp.transpose(state, (2, 0, 1, 3, 4))

    def evolve(level):
        for sub in range(NSUB):
            padded = fill_cycle(level, edge_rotation)
            height, east, north = advance(padded[:, 0], padded[:, 1], padded[:, 2], coriolis)
            level = jnp.stack([height, east, north], axis=1)
        return level

    after = jnp.transpose(lax.map(evolve, levels_first), (1, 2, 0, 3, 4))

    def lines(field):
        shaped = field.reshape(2, 3, LEVEL_COUNT, FIRST_DIM_LINES, TILE, NY)
        return jnp.transpose(shaped, (0, 3, 1, 2, 4, 5)).reshape(2 * FIRST_DIM_LINES, 3, LEVEL_COUNT, TILE, NY)

    source_tiles = parent_tile_index.reshape(2 * FIRST_DIM_LINES, LINE_NEST_BLOCKS).astype(jnp.int32)
    block_spots = parent_spot_index.reshape(2 * FIRST_DIM_LINES, LINE_NEST_BLOCKS).astype(jnp.int32)
    every_block = nest_block_state.reshape(2 * FIRST_DIM_LINES, LINE_NEST_BLOCKS, 3, LEVEL_COUNT, NEST_CELLS2)

    def per_line(items):
        start_line, after_line, line_sources, line_places, blocks = items
        rows = (line_sources * BLOCK_SPOTS + line_places).astype(jnp.int32)
        start_rows = line_rows(start_line)
        after_rows = line_rows(after_line)
        blocks_out = blend_nest(blocks, start_rows[rows])
        means = block_means(blocks_out)
        change = BETA * (means - after_rows[rows])
        after_rows = after_rows + jnp.zeros_like(after_rows).at[rows].add(change)
        return blocks_out, line_field(after_rows)

    nested_line_list, final_lines = lax.map(per_line, (lines(state), lines(after), source_tiles, block_spots, every_block))
    final_result = jnp.transpose(final_lines.reshape(2, FIRST_DIM_LINES, 3, LEVEL_COUNT, TILE, NY), (0, 2, 3, 1, 4, 5)).reshape(2, 3, LEVEL_COUNT, NX, NY)
    return final_result, nested_line_list.reshape(2, FIRST_DIM_LINES, LINE_NEST_BLOCKS, 3, LEVEL_COUNT, NEST_CELLS2)
```

```python
import jax
import jax.numpy as jnp
from jax import lax
from jax.sharding import PartitionSpec as P

NSUB = 2
PATCH = 8
RATIO = 3
FINE = 24


DT_STEP = 0.25
GRAVITY = 1.0
DAMPING = 0.5
DEPTH = 1.0
KAPPA = 0.2
ALPHA = 0.5
BETA = 0.5

HI = lax.Precision.HIGHEST


def shift_pairs(count, step):
    return [(i, i + step) for i in range(count) if 0 <= i + step < count]


def rotated(code, east_part, north_part):
    along = (code == 0).astype(east_part.dtype) - (code == 2).astype(east_part.dtype)
    across = (code == 3).astype(east_part.dtype) - (code == 1).astype(east_part.dtype)
    return (along * east_part + across * north_part, along * north_part - across * east_part)


def centre(field):
    return field[..., 1:-1, 1:-1]


def along_x(field):
    return 0.5 * (field[..., 2:, 1:-1] - field[..., :-2, 1:-1])


def along_y(field):
    return 0.5 * (field[..., 1:-1, 2:] - field[..., 1:-1, :-2])


def laplacian(field):
    return (
        field[..., 2:, 1:-1]
        + field[..., :-2, 1:-1]
        + field[..., 1:-1, 2:]
        + field[..., 1:-1, :-2]
        - 4.0 * centre(field)
    )


def advance(height, east, north, coriolis):
    absolute = coriolis + along_x(north) - along_y(east)
    depth = DEPTH + height
    divergence = along_x(depth * east) + along_y(depth * north)
    new_height = centre(height) - DT_STEP * divergence
    new_east = centre(east) + DT_STEP * (
        absolute * centre(north) - GRAVITY * along_x(height) + DAMPING * laplacian(east)
    )
    new_north = centre(north) + DT_STEP * (
        -absolute * centre(east) - GRAVITY * along_y(height) + DAMPING * laplacian(north)
    )
    return (new_height, new_east, new_north)


def padded_field(field, west, east, south, north):
    rows = jnp.concatenate([west[:, None, :], field, east[:, None, :]], axis=1)
    zero = jnp.zeros_like(south[:, :1])
    low = jnp.concatenate([zero, south, zero], axis=1)[:, :, None]
    high = jnp.concatenate([zero, north, zero], axis=1)[:, :, None]
    return jnp.concatenate([low, rows, high], axis=2)


def substep(fields, coriolis, codes, flags):
    nx = lax.axis_size("gx")
    ny = lax.axis_size("gy")
    first_rows = jnp.stack([f[:, 0, :] for f in fields], axis=0)
    last_rows = jnp.stack([f[:, -1, :] for f in fields], axis=0)
    first_cols = jnp.stack([f[:, :, 0] for f in fields], axis=0)
    last_cols = jnp.stack([f[:, :, -1] for f in fields], axis=0)
    from_west = lax.ppermute(last_rows, "gx", shift_pairs(nx, 1))
    from_east = lax.ppermute(first_rows, "gx", shift_pairs(nx, -1))
    from_south = lax.ppermute(last_cols, "gy", shift_pairs(ny, 1))
    from_north = lax.ppermute(first_cols, "gy", shift_pairs(ny, -1))
    strips = jnp.stack([first_rows, last_rows, first_cols, last_cols], axis=0)
    partner = lax.ppermute(strips, "panel", [(0, 1), (1, 0)])
    halos = []
    for side, neighbour in enumerate((from_west, from_east, from_south, from_north)):
        strip = partner[side]
        east_rot, north_rot = rotated(codes[side], strip[1], strip[2])
        strip = jnp.stack([strip[0], east_rot, north_rot], axis=0)
        halos.append(jnp.where(flags[side], strip, neighbour))
    padded = [padded_field(fields[c], *(h[c] for h in halos)) for c in range(3)]
    return advance(padded[0], padded[1], padded[2], coriolis)


def body(state, coriolis, edge_rotation, nest_block_state, parent_tile_index, parent_spot_index):
    devices_y = lax.axis_size("gy")
    slots = nest_block_state.shape[2]
    capacity = 2
    width = devices_y * capacity
    my_row = lax.axis_index("gy")
    my_column = lax.axis_index("gx")
    tile = state[0]
    level_stack = tile.shape[1]
    side_x = tile.shape[2]
    side_y = tile.shape[3]
    qy = side_y // PATCH
    cells = 3 * level_stack * PATCH * PATCH

    mine = parent_tile_index.reshape(slots)
    spots = parent_spot_index.reshape(slots)
    local = jnp.arange(slots, dtype=jnp.int32)
    rank = jnp.sum(
        ((mine[:, None] == mine[None, :]) & (local[None, :] < local[:, None])).astype(jnp.int32),
        axis=1,
    )
    slot_of = mine * capacity + rank
    slot_hit = jnp.arange(width, dtype=jnp.int32)[:, None] == slot_of[None, :]
    request = jnp.sum(jnp.where(slot_hit, spots[None, :] + 1, 0), axis=1) - 1
    asked = lax.all_to_all(
        request.reshape(devices_y, capacity), "gy", split_axis=0, concat_axis=0, tiled=True
    ).reshape(width)

    valid = asked >= 0
    row0 = (asked // qy) * PATCH
    col0 = (asked % qy) * PATCH
    offs = jnp.arange(PATCH, dtype=jnp.int32)
    rows_at = jnp.arange(side_x, dtype=jnp.int32)
    cols_at = jnp.arange(side_y, dtype=jnp.int32)
    row_sel = (
        (rows_at[None, None, :] == (row0[:, None, None] + offs[None, :, None]))
        & valid[:, None, None]
    ).astype(jnp.float32)
    col_sel = (cols_at[None, None, :] == (col0[:, None, None] + offs[None, :, None])).astype(
        jnp.float32
    )
    picked_rows = jnp.einsum("kar,flrc->kflac", row_sel, tile, precision=HI)
    picked = jnp.einsum("kflac,kbc->kflab", picked_rows, col_sel, precision=HI)
    incoming = lax.all_to_all(
        picked.reshape(devices_y, capacity, cells), "gy", split_axis=0, concat_axis=0, tiled=True
    ).reshape(width, cells)

    parent = jnp.take(incoming, slot_of, axis=0)
    fine_cells = FINE * FINE
    coarse_cells = PATCH * PATCH
    n_idx = jnp.arange(fine_cells, dtype=jnp.int32)
    fi = n_idx // FINE
    fj = n_idx % FINE
    coarse_of = (fi // RATIO) * PATCH + (fj // RATIO)
    m_idx = jnp.arange(coarse_cells, dtype=jnp.int32)
    spread = (m_idx[:, None] == coarse_of[None, :]).astype(jnp.float32)
    coarse = parent.reshape(slots * 3 * level_stack, coarse_cells)
    upsampled = jnp.dot(coarse, spread, precision=HI)
    blocks = nest_block_state[0, 0].reshape(slots * 3 * level_stack, fine_cells)
    pad_lo = jnp.concatenate([blocks[:, :FINE], blocks[:, :-FINE]], axis=1)
    pad_hi = jnp.concatenate([blocks[:, FINE:], blocks[:, -FINE:]], axis=1)
    left = jnp.concatenate([blocks[:, :1], blocks[:, :-1]], axis=1)
    right = jnp.concatenate([blocks[:, 1:], blocks[:, -1:]], axis=1)
    left = jnp.where((fj == 0)[None, :], blocks, left)
    right = jnp.where((fj == FINE - 1)[None, :], blocks, right)
    lap = pad_hi + pad_lo + right + left - 4.0 * blocks
    smoothed = blocks + KAPPA * lap
    blended = smoothed + ALPHA * (upsampled - smoothed)
    sums = jnp.dot(blended, spread.T, precision=HI)
    means = (sums / float(RATIO * RATIO)).reshape(slots, cells)
    back = jnp.dot(slot_hit.astype(jnp.float32), means, precision=HI)
    returned = lax.all_to_all(
        back.reshape(devices_y, capacity, cells), "gy", split_axis=0, concat_axis=0, tiled=True
    ).reshape(width, 3, level_stack, PATCH, PATCH)

    codes = edge_rotation[0]
    flags = [
        my_column == 0,
        my_column == lax.axis_size("gx") - 1,
        my_row == 0,
        my_row == devices_y - 1,
    ]
    fields = (tile[0], tile[1], tile[2])
    cell_coriolis = coriolis[0][None]
    for sub in range(NSUB):
        fields = substep(fields, cell_coriolis, codes, flags)

    spread_cols = jnp.einsum("kflab,kbc->kflac", returned, col_sel, precision=HI)
    dense = jnp.einsum("kar,kflac->flrc", row_sel, spread_cols, precision=HI)
    row_mask = jnp.sum(row_sel, axis=1)
    col_mask = jnp.sum(col_sel, axis=1)
    count = jnp.dot(row_mask.T, col_mask, precision=HI)
    after = jnp.stack(fields, axis=0)
    final_result = after + BETA * (dense - count[None, None] * after)
    return (final_result[None], blended.reshape(1, 1, slots, 3, level_stack, fine_cells))


def solution(mesh):
    in_specs = (
        P("panel", None, None, "gx", "gy"),
        P("panel", "gx", "gy"),
        P("panel", None),
        P("panel", "gx", "gy", None, None, None),
        P("panel", "gx", "gy", None),
        P("panel", "gx", "gy"),
    )
    out_specs = (P("panel", None, None, "gx", "gy"), P("panel", "gx", "gy", None, None, None))
    return jax.shard_map(body, mesh=mesh, in_specs=in_specs, out_specs=out_specs, check_vma=False)
```

```python
import jax
import jax.numpy as jnp
from jax import lax
from jax.sharding import PartitionSpec as P

NSUB = 2
PATCH = 8
RATIO = 3
FINE = 24


DT_STEP = 0.25
GRAVITY = 1.0
DAMPING = 0.5
DEPTH = 1.0
KAPPA = 0.2
ALPHA = 0.5
BETA = 0.5

HI = lax.Precision.HIGHEST


def shift_pairs(count, step):
    return [(i, i + step) for i in range(count) if 0 <= i + step < count]


def rotated(code, east_part, north_part):
    along = (code == 0).astype(east_part.dtype) - (code == 2).astype(east_part.dtype)
    across = (code == 3).astype(east_part.dtype) - (code == 1).astype(east_part.dtype)
    return (along * east_part + across * north_part, along * north_part - across * east_part)


def centre(field):
    return field[..., 1:-1, 1:-1]


def along_x(field):
    return 0.5 * (field[..., 2:, 1:-1] - field[..., :-2, 1:-1])


def along_y(field):
    return 0.5 * (field[..., 1:-1, 2:] - field[..., 1:-1, :-2])


def laplacian(field):
    return (
        field[..., 2:, 1:-1]
        + field[..., :-2, 1:-1]
        + field[..., 1:-1, 2:]
        + field[..., 1:-1, :-2]
        - 4.0 * centre(field)
    )


def advance(height, east, north, coriolis):
    absolute = coriolis + along_x(north) - along_y(east)
    depth = DEPTH + height
    divergence = along_x(depth * east) + along_y(depth * north)
    new_height = centre(height) - DT_STEP * divergence
    new_east = centre(east) + DT_STEP * (
        absolute * centre(north) - GRAVITY * along_x(height) + DAMPING * laplacian(east)
    )
    new_north = centre(north) + DT_STEP * (
        -absolute * centre(east) - GRAVITY * along_y(height) + DAMPING * laplacian(north)
    )
    return (new_height, new_east, new_north)


def padded_field(field, west, east, south, north):
    rows = jnp.concatenate([west[:, None, :], field, east[:, None, :]], axis=1)
    zero = jnp.zeros_like(south[:, :1])
    low = jnp.concatenate([zero, south, zero], axis=1)[:, :, None]
    high = jnp.concatenate([zero, north, zero], axis=1)[:, :, None]
    return jnp.concatenate([low, rows, high], axis=2)


def ring_pairs(count):
    pairs = [(g, g + 1) for g in range(count - 1)]
    pairs.append((count - 1, 2 * count - 1))
    pairs += [(count + g, count + g - 1) for g in range(1, count)]
    pairs.append((count, 0))
    return pairs


def ring_exchange(first, last, axis, on_first_panel):
    count = lax.axis_size(axis)
    forward = ring_pairs(count)
    backward = [(target, source) for source, target in forward]
    sent_forward = jnp.where(on_first_panel, last, first)
    sent_backward = jnp.where(on_first_panel, first, last)
    got_forward = lax.ppermute(sent_forward, ("panel", axis), forward)
    got_backward = lax.ppermute(sent_backward, ("panel", axis), backward)
    low = jnp.where(on_first_panel, got_forward, got_backward)
    high = jnp.where(on_first_panel, got_backward, got_forward)
    return low, high


def edge_fix(strip, code, flag):
    east_rot, north_rot = rotated(code, strip[1], strip[2])
    turned = jnp.stack([strip[0], east_rot, north_rot], axis=0)
    return jnp.where(flag, turned, strip)


def substep(fields, coriolis, codes, flags, on_first_panel):
    first_rows = jnp.stack([f[:, 0, :] for f in fields], axis=0)
    last_rows = jnp.stack([f[:, -1, :] for f in fields], axis=0)
    first_cols = jnp.stack([f[:, :, 0] for f in fields], axis=0)
    last_cols = jnp.stack([f[:, :, -1] for f in fields], axis=0)
    west, east = ring_exchange(first_rows, last_rows, "gx", on_first_panel)
    south, north = ring_exchange(first_cols, last_cols, "gy", on_first_panel)
    halos = [
        edge_fix(strip, codes[side], flags[side])
        for side, strip in enumerate((west, east, south, north))
    ]
    padded = [padded_field(fields[c], *(h[c] for h in halos)) for c in range(3)]
    return advance(padded[0], padded[1], padded[2], coriolis)


def body(state, coriolis, edge_rotation, nest_block_state, parent_tile_index, parent_spot_index):
    devices_y = lax.axis_size("gy")
    slots = nest_block_state.shape[2]
    capacity = 2
    width = devices_y * capacity
    my_row = lax.axis_index("gy")
    my_column = lax.axis_index("gx")
    on_first_panel = lax.axis_index("panel") == 0
    tile = state[0]
    level_stack = tile.shape[1]
    side_x = tile.shape[2]
    side_y = tile.shape[3]
    qy = side_y // PATCH
    cells = 3 * level_stack * PATCH * PATCH
    fine_cells = FINE * FINE
    coarse_cells = PATCH * PATCH

    n_idx = jnp.arange(fine_cells, dtype=jnp.int32)
    fi = n_idx // FINE
    fj = n_idx % FINE
    coarse_of = (fi // RATIO) * PATCH + (fj // RATIO)
    m_idx = jnp.arange(coarse_cells, dtype=jnp.int32)
    spread = (m_idx[:, None] == coarse_of[None, :]).astype(jnp.float32)
    blocks = nest_block_state[0, 0].reshape(slots * 3 * level_stack, fine_cells)
    pad_lo = jnp.concatenate([blocks[:, :FINE], blocks[:, :-FINE]], axis=1)
    pad_hi = jnp.concatenate([blocks[:, FINE:], blocks[:, -FINE:]], axis=1)
    left = jnp.concatenate([blocks[:, :1], blocks[:, :-1]], axis=1)
    right = jnp.concatenate([blocks[:, 1:], blocks[:, -1:]], axis=1)
    left = jnp.where((fj == 0)[None, :], blocks, left)
    right = jnp.where((fj == FINE - 1)[None, :], blocks, right)
    lap = pad_hi + pad_lo + right + left - 4.0 * blocks
    smoothed = blocks + KAPPA * lap
    smooth_means = (jnp.dot(smoothed, spread.T, precision=HI) / float(RATIO * RATIO)).reshape(
        slots, cells
    )

    mine = parent_tile_index.reshape(slots)
    spots = parent_spot_index.reshape(slots)
    local = jnp.arange(slots, dtype=jnp.int32)
    rank = jnp.sum(
        ((mine[:, None] == mine[None, :]) & (local[None, :] < local[:, None])).astype(jnp.int32),
        axis=1,
    )
    slot_of = mine * capacity + rank
    slot_hit = (jnp.arange(width, dtype=jnp.int32)[:, None] == slot_of[None, :]).astype(
        jnp.float32
    )
    payload = jnp.concatenate(
        [(spots + 1).astype(jnp.float32)[:, None], smooth_means], axis=1
    )
    outgoing = jnp.dot(slot_hit, payload, precision=HI)
    asked_payload = lax.all_to_all(
        outgoing.reshape(devices_y, capacity, cells + 1), "gy", split_axis=0, concat_axis=0,
        tiled=True,
    ).reshape(width, cells + 1)
    asked = asked_payload[:, 0].astype(jnp.int32) - 1
    asked_means = asked_payload[:, 1:].reshape(width, 3, level_stack, PATCH, PATCH)

    valid = asked >= 0
    row0 = (asked // qy) * PATCH
    col0 = (asked % qy) * PATCH
    offs = jnp.arange(PATCH, dtype=jnp.int32)
    rows_at = jnp.arange(side_x, dtype=jnp.int32)
    cols_at = jnp.arange(side_y, dtype=jnp.int32)
    row_sel = (
        (rows_at[None, None, :] == (row0[:, None, None] + offs[None, :, None]))
        & valid[:, None, None]
    ).astype(jnp.float32)
    col_sel = (cols_at[None, None, :] == (col0[:, None, None] + offs[None, :, None])).astype(
        jnp.float32
    )
    picked_rows = jnp.einsum("kar,flrc->kflac", row_sel, tile, precision=HI)
    picked = jnp.einsum("kflac,kbc->kflab", picked_rows, col_sel, precision=HI)
    incoming = lax.all_to_all(
        picked.reshape(devices_y, capacity, cells), "gy", split_axis=0, concat_axis=0, tiled=True
    ).reshape(width, cells)

    parent = jnp.take(incoming, slot_of, axis=0)
    coarse = parent.reshape(slots * 3 * level_stack, coarse_cells)
    upsampled = jnp.dot(coarse, spread, precision=HI)
    blended = smoothed + ALPHA * (upsampled - smoothed)

    codes = edge_rotation[0]
    flags = [
        my_column == 0,
        my_column == lax.axis_size("gx") - 1,
        my_row == 0,
        my_row == devices_y - 1,
    ]
    fields = (tile[0], tile[1], tile[2])
    cell_coriolis = coriolis[0][None]
    for sub in range(NSUB):
        fields = substep(fields, cell_coriolis, codes, flags, on_first_panel)

    block_mean = asked_means + ALPHA * (picked - asked_means)
    spread_cols = jnp.einsum("kflab,kbc->kflac", block_mean, col_sel, precision=HI)
    dense = jnp.einsum("kar,kflac->flrc", row_sel, spread_cols, precision=HI)
    row_mask = jnp.sum(row_sel, axis=1)
    col_mask = jnp.sum(col_sel, axis=1)
    count = jnp.dot(row_mask.T, col_mask, precision=HI)
    after = jnp.stack(fields, axis=0)
    final_result = after + BETA * (dense - count[None, None] * after)
    return (final_result[None], blended.reshape(1, 1, slots, 3, level_stack, fine_cells))


def solution(mesh):
    in_specs = (
        P("panel", None, None, "gx", "gy"),
        P("panel", "gx", "gy"),
        P("panel", None),
        P("panel", "gx", "gy", None, None, None),
        P("panel", "gx", "gy", None),
        P("panel", "gx", "gy"),
    )
    out_specs = (P("panel", None, None, "gx", "gy"), P("panel", "gx", "gy", None, None, None))
    return jax.shard_map(body, mesh=mesh, in_specs=in_specs, out_specs=out_specs, check_vma=False)
```

```python
import jax
import jax.numpy as jnp
from jax import lax
from jax.sharding import PartitionSpec as P

NSUB = 2
PATCH = 8
RATIO = 3
FINE = 24


DT_STEP = 0.25
GRAVITY = 1.0
DAMPING = 0.5
DEPTH = 1.0
KAPPA = 0.2
ALPHA = 0.5
BETA = 0.5

HI = lax.Precision.HIGHEST


def shift_pairs(count, step):
    return [(i, i + step) for i in range(count) if 0 <= i + step < count]


def rotated(code, east_part, north_part):
    along = (code == 0).astype(east_part.dtype) - (code == 2).astype(east_part.dtype)
    across = (code == 3).astype(east_part.dtype) - (code == 1).astype(east_part.dtype)
    return (along * east_part + across * north_part, along * north_part - across * east_part)


def centre(field):
    return field[..., 1:-1, 1:-1]


def along_x(field):
    return 0.5 * (field[..., 2:, 1:-1] - field[..., :-2, 1:-1])


def along_y(field):
    return 0.5 * (field[..., 1:-1, 2:] - field[..., 1:-1, :-2])


def laplacian(field):
    return (
        field[..., 2:, 1:-1]
        + field[..., :-2, 1:-1]
        + field[..., 1:-1, 2:]
        + field[..., 1:-1, :-2]
        - 4.0 * centre(field)
    )


def advance(height, east, north, coriolis):
    absolute = coriolis + along_x(north) - along_y(east)
    depth = DEPTH + height
    divergence = along_x(depth * east) + along_y(depth * north)
    new_height = centre(height) - DT_STEP * divergence
    new_east = centre(east) + DT_STEP * (
        absolute * centre(north) - GRAVITY * along_x(height) + DAMPING * laplacian(east)
    )
    new_north = centre(north) + DT_STEP * (
        -absolute * centre(east) - GRAVITY * along_y(height) + DAMPING * laplacian(north)
    )
    return (new_height, new_east, new_north)


def padded_field(field, west, east, south, north):
    rows = jnp.concatenate([west[:, None, :], field, east[:, None, :]], axis=1)
    zero = jnp.zeros_like(south[:, :1])
    low = jnp.concatenate([zero, south, zero], axis=1)[:, :, None]
    high = jnp.concatenate([zero, north, zero], axis=1)[:, :, None]
    return jnp.concatenate([low, rows, high], axis=2)


def ring_pairs(count):
    pairs = [(g, g + 1) for g in range(count - 1)]
    pairs.append((count - 1, 2 * count - 1))
    pairs += [(count + g, count + g - 1) for g in range(1, count)]
    pairs.append((count, 0))
    return pairs


def ring_exchange(first, last, axis, on_first_panel):
    count = lax.axis_size(axis)
    forward = ring_pairs(count)
    backward = [(target, source) for source, target in forward]
    sent_forward = jnp.where(on_first_panel, last, first)
    sent_backward = jnp.where(on_first_panel, first, last)
    got_forward = lax.ppermute(sent_forward, ("panel", axis), forward)
    got_backward = lax.ppermute(sent_backward, ("panel", axis), backward)
    low = jnp.where(on_first_panel, got_forward, got_backward)
    high = jnp.where(on_first_panel, got_backward, got_forward)
    return low, high


def edge_turns(codes, flags):
    along = (codes == 0).astype(jnp.float32) - (codes == 2).astype(jnp.float32)
    across = (codes == 3).astype(jnp.float32) - (codes == 1).astype(jnp.float32)
    crossing = jnp.stack(flags)
    along = jnp.where(crossing, along, 1.0)
    across = jnp.where(crossing, across, 0.0)
    one = jnp.ones_like(along)
    zero = jnp.zeros_like(along)
    return jnp.stack(
        [
            jnp.stack([one, zero, zero], axis=1),
            jnp.stack([zero, along, across], axis=1),
            jnp.stack([zero, -across, along], axis=1),
        ],
        axis=1,
    )


def substep(fields, coriolis, turns, on_first_panel):
    first_rows = jnp.stack([f[:, 0, :] for f in fields], axis=0)
    last_rows = jnp.stack([f[:, -1, :] for f in fields], axis=0)
    first_cols = jnp.stack([f[:, :, 0] for f in fields], axis=0)
    last_cols = jnp.stack([f[:, :, -1] for f in fields], axis=0)
    west, east = ring_exchange(first_rows, last_rows, "gx", on_first_panel)
    south, north = ring_exchange(first_cols, last_cols, "gy", on_first_panel)
    strips = jnp.stack([west, east, south, north], axis=0)
    halos = jnp.einsum("sij,sjlc->silc", turns, strips, precision=HI)
    padded = [padded_field(fields[c], *(h[c] for h in halos)) for c in range(3)]
    return advance(padded[0], padded[1], padded[2], coriolis)


def body(state, coriolis, edge_rotation, nest_block_state, parent_tile_index, parent_spot_index):
    devices_y = lax.axis_size("gy")
    slots = nest_block_state.shape[2]
    capacity = 2
    width = devices_y * capacity
    my_row = lax.axis_index("gy")
    my_column = lax.axis_index("gx")
    on_first_panel = lax.axis_index("panel") == 0
    tile = state[0]
    level_stack = tile.shape[1]
    side_x = tile.shape[2]
    side_y = tile.shape[3]
    qy = side_y // PATCH
    cells = 3 * level_stack * PATCH * PATCH
    fine_cells = FINE * FINE
    coarse_cells = PATCH * PATCH

    n_idx = jnp.arange(fine_cells, dtype=jnp.int32)
    fi = n_idx // FINE
    fj = n_idx % FINE
    coarse_of = (fi // RATIO) * PATCH + (fj // RATIO)
    m_idx = jnp.arange(coarse_cells, dtype=jnp.int32)
    spread = (m_idx[:, None] == coarse_of[None, :]).astype(jnp.float32)
    blocks = nest_block_state[0, 0].reshape(slots * 3 * level_stack, fine_cells)
    pad_lo = jnp.concatenate([blocks[:, :FINE], blocks[:, :-FINE]], axis=1)
    pad_hi = jnp.concatenate([blocks[:, FINE:], blocks[:, -FINE:]], axis=1)
    left = jnp.concatenate([blocks[:, :1], blocks[:, :-1]], axis=1)
    right = jnp.concatenate([blocks[:, 1:], blocks[:, -1:]], axis=1)
    left = jnp.where((fj == 0)[None, :], blocks, left)
    right = jnp.where((fj == FINE - 1)[None, :], blocks, right)
    lap = pad_hi + pad_lo + right + left - 4.0 * blocks
    smoothed = blocks + KAPPA * lap
    smooth_means = (jnp.dot(smoothed, spread.T, precision=HI) / float(RATIO * RATIO)).reshape(
        slots, cells
    )

    mine = parent_tile_index.reshape(slots)
    spots = parent_spot_index.reshape(slots)
    local = jnp.arange(slots, dtype=jnp.int32)
    rank = jnp.sum(
        ((mine[:, None] == mine[None, :]) & (local[None, :] < local[:, None])).astype(jnp.int32),
        axis=1,
    )
    slot_of = mine * capacity + rank
    slot_hit = (jnp.arange(width, dtype=jnp.int32)[:, None] == slot_of[None, :]).astype(
        jnp.float32
    )
    payload = jnp.concatenate(
        [(spots + 1).astype(jnp.float32)[:, None], smooth_means], axis=1
    )
    outgoing = jnp.dot(slot_hit, payload, precision=HI)
    asked_payload = lax.all_to_all(
        outgoing.reshape(devices_y, capacity, cells + 1), "gy", split_axis=0, concat_axis=0,
        tiled=True,
    ).reshape(width, cells + 1)
    asked = asked_payload[:, 0].astype(jnp.int32) - 1
    asked_means = asked_payload[:, 1:].reshape(width, 3, level_stack, PATCH, PATCH)

    valid = asked >= 0
    row0 = (asked // qy) * PATCH
    col0 = (asked % qy) * PATCH
    offs = jnp.arange(PATCH, dtype=jnp.int32)
    rows_at = jnp.arange(side_x, dtype=jnp.int32)
    cols_at = jnp.arange(side_y, dtype=jnp.int32)
    row_sel = (
        (rows_at[None, None, :] == (row0[:, None, None] + offs[None, :, None]))
        & valid[:, None, None]
    ).astype(jnp.float32)
    col_sel = (cols_at[None, None, :] == (col0[:, None, None] + offs[None, :, None])).astype(
        jnp.float32
    )
    picked_rows = jnp.einsum("kar,flrc->kflac", row_sel, tile, precision=HI)
    picked = jnp.einsum("kflac,kbc->kflab", picked_rows, col_sel, precision=HI)
    incoming = lax.all_to_all(
        picked.reshape(devices_y, capacity, cells), "gy", split_axis=0, concat_axis=0, tiled=True
    ).reshape(width, cells)

    parent = jnp.take(incoming, slot_of, axis=0)
    coarse = parent.reshape(slots * 3 * level_stack, coarse_cells)
    upsampled = jnp.dot(coarse, spread, precision=HI)
    blended = smoothed + ALPHA * (upsampled - smoothed)

    codes = edge_rotation[0]
    flags = [
        my_column == 0,
        my_column == lax.axis_size("gx") - 1,
        my_row == 0,
        my_row == devices_y - 1,
    ]
    turns = edge_turns(codes, flags)
    fields = (tile[0], tile[1], tile[2])
    cell_coriolis = coriolis[0][None]
    for sub in range(NSUB):
        fields = substep(fields, cell_coriolis, turns, on_first_panel)

    block_mean = asked_means + ALPHA * (picked - asked_means)
    spread_cols = jnp.einsum("kflab,kbc->kflac", block_mean, col_sel, precision=HI)
    dense = jnp.einsum("kar,kflac->flrc", row_sel, spread_cols, precision=HI)
    row_mask = jnp.sum(row_sel, axis=1)
    col_mask = jnp.sum(col_sel, axis=1)
    count = jnp.dot(row_mask.T, col_mask, precision=HI)
    after = jnp.stack(fields, axis=0)
    final_result = after + BETA * (dense - count[None, None] * after)
    return (final_result[None], blended.reshape(1, 1, slots, 3, level_stack, fine_cells))


def solution(mesh):
    in_specs = (
        P("panel", None, None, "gx", "gy"),
        P("panel", "gx", "gy"),
        P("panel", None),
        P("panel", "gx", "gy", None, None, None),
        P("panel", "gx", "gy", None),
        P("panel", "gx", "gy"),
    )
    out_specs = (P("panel", None, None, "gx", "gy"), P("panel", "gx", "gy", None, None, None))
    return jax.shard_map(body, mesh=mesh, in_specs=in_specs, out_specs=out_specs, check_vma=False)
```

```python
import jax
import jax.numpy as jnp
from jax import lax
from jax.sharding import PartitionSpec as P

NSUB = 2
PATCH = 8
RATIO = 3
FINE = 24


DT_STEP = 0.25
GRAVITY = 1.0
DAMPING = 0.5
DEPTH = 1.0
KAPPA = 0.2
ALPHA = 0.5
BETA = 0.5

HI = lax.Precision.HIGHEST


def centre(field):
    return field[..., 1:-1, 1:-1]


def along_x(field):
    return 0.5 * (field[..., 2:, 1:-1] - field[..., :-2, 1:-1])


def along_y(field):
    return 0.5 * (field[..., 1:-1, 2:] - field[..., 1:-1, :-2])


def laplacian(field):
    return (
        field[..., 2:, 1:-1]
        + field[..., :-2, 1:-1]
        + field[..., 1:-1, 2:]
        + field[..., 1:-1, :-2]
        - 4.0 * centre(field)
    )


def advance(height, east, north, coriolis):
    absolute = coriolis + along_x(north) - along_y(east)
    depth = DEPTH + height
    divergence = along_x(depth * east) + along_y(depth * north)
    new_height = centre(height) - DT_STEP * divergence
    new_east = centre(east) + DT_STEP * (
        absolute * centre(north) - GRAVITY * along_x(height) + DAMPING * laplacian(east)
    )
    new_north = centre(north) + DT_STEP * (
        -absolute * centre(east) - GRAVITY * along_y(height) + DAMPING * laplacian(north)
    )
    return (new_height, new_east, new_north)


def padded_field(field, west, east, south, north):
    rows = jnp.concatenate([west[:, None, :], field, east[:, None, :]], axis=1)
    zero = jnp.zeros_like(south[:, :1])
    low = jnp.concatenate([zero, south, zero], axis=1)[:, :, None]
    high = jnp.concatenate([zero, north, zero], axis=1)[:, :, None]
    return jnp.concatenate([low, rows, high], axis=2)


def ring_pairs(count):
    pairs = [(g, g + 1) for g in range(count - 1)]
    pairs.append((count - 1, 2 * count - 1))
    pairs += [(count + g, count + g - 1) for g in range(1, count)]
    pairs.append((count, 0))
    return pairs


def ring_exchange(first, last, axis, on_first_panel):
    count = lax.axis_size(axis)
    forward = ring_pairs(count)
    backward = [(target, source) for source, target in forward]
    sent_forward = jnp.where(on_first_panel, last, first)
    sent_backward = jnp.where(on_first_panel, first, last)
    got_forward = lax.ppermute(sent_forward, ("panel", axis), forward)
    got_backward = lax.ppermute(sent_backward, ("panel", axis), backward)
    low = jnp.where(on_first_panel, got_forward, got_backward)
    high = jnp.where(on_first_panel, got_backward, got_forward)
    return low, high


def edge_turns(codes, flags):
    along = (codes == 0).astype(jnp.float32) - (codes == 2).astype(jnp.float32)
    across = (codes == 3).astype(jnp.float32) - (codes == 1).astype(jnp.float32)
    crossing = jnp.stack(flags)
    along = jnp.where(crossing, along, 1.0)
    across = jnp.where(crossing, across, 0.0)
    one = jnp.ones_like(along)
    zero = jnp.zeros_like(along)
    return jnp.stack(
        [
            jnp.stack([one, zero, zero], axis=1),
            jnp.stack([zero, along, across], axis=1),
            jnp.stack([zero, -across, along], axis=1),
        ],
        axis=1,
    )


def substep(fields, coriolis, turns, on_first_panel):
    first_rows = jnp.stack([f[:, 0, :] for f in fields], axis=0)
    last_rows = jnp.stack([f[:, -1, :] for f in fields], axis=0)
    first_cols = jnp.stack([f[:, :, 0] for f in fields], axis=0)
    last_cols = jnp.stack([f[:, :, -1] for f in fields], axis=0)
    west, east = ring_exchange(first_rows, last_rows, "gx", on_first_panel)
    south, north = ring_exchange(first_cols, last_cols, "gy", on_first_panel)
    strips = jnp.stack([west, east, south, north], axis=0)
    halos = jnp.einsum("sij,sjlc->silc", turns, strips, precision=HI)
    padded = [padded_field(fields[c], *(h[c] for h in halos)) for c in range(3)]
    return advance(padded[0], padded[1], padded[2], coriolis)


def step(state, coriolis, edge_rotation, nest_block_state, parent_tile_index, parent_spot_index):
    devices_y = lax.axis_size("gy")
    slots = nest_block_state.shape[2]
    capacity = 2
    width = devices_y * capacity
    my_row = lax.axis_index("gy")
    my_column = lax.axis_index("gx")
    on_first_panel = lax.axis_index("panel") == 0
    tile = state[0]
    level_stack = tile.shape[1]
    side_x = tile.shape[2]
    side_y = tile.shape[3]
    qy = side_y // PATCH
    cells = 3 * level_stack * PATCH * PATCH
    fine_cells = FINE * FINE
    coarse_cells = PATCH * PATCH

    n_idx = jnp.arange(fine_cells, dtype=jnp.int32)
    fi = n_idx // FINE
    fj = n_idx % FINE
    coarse_of = (fi // RATIO) * PATCH + (fj // RATIO)
    m_idx = jnp.arange(coarse_cells, dtype=jnp.int32)
    spread = (m_idx[:, None] == coarse_of[None, :]).astype(jnp.float32)
    blocks = nest_block_state[0, 0].reshape(slots * 3 * level_stack, fine_cells)
    pad_lo = jnp.concatenate([blocks[:, :FINE], blocks[:, :-FINE]], axis=1)
    pad_hi = jnp.concatenate([blocks[:, FINE:], blocks[:, -FINE:]], axis=1)
    left = jnp.concatenate([blocks[:, :1], blocks[:, :-1]], axis=1)
    right = jnp.concatenate([blocks[:, 1:], blocks[:, -1:]], axis=1)
    left = jnp.where((fj == 0)[None, :], blocks, left)
    right = jnp.where((fj == FINE - 1)[None, :], blocks, right)
    lap = pad_hi + pad_lo + right + left - 4.0 * blocks
    smoothed = blocks + KAPPA * lap
    smooth_means = (jnp.dot(smoothed, spread.T, precision=HI) / float(RATIO * RATIO)).reshape(
        slots, cells
    )

    mine = parent_tile_index.reshape(slots)
    spots = parent_spot_index.reshape(slots)
    local = jnp.arange(slots, dtype=jnp.int32)
    rank = jnp.sum(
        ((mine[:, None] == mine[None, :]) & (local[None, :] < local[:, None])).astype(jnp.int32),
        axis=1,
    )
    slot_of = mine * capacity + rank
    slot_hit = (jnp.arange(width, dtype=jnp.int32)[:, None] == slot_of[None, :]).astype(
        jnp.float32
    )
    payload = jnp.concatenate(
        [(spots + 1).astype(jnp.float32)[:, None], smooth_means], axis=1
    )
    outgoing = jnp.dot(slot_hit, payload, precision=HI)
    asked_payload = lax.all_to_all(
        outgoing.reshape(devices_y, capacity, cells + 1), "gy", split_axis=0, concat_axis=0,
        tiled=True,
    ).reshape(width, cells + 1)
    asked = asked_payload[:, 0].astype(jnp.int32) - 1
    asked_means = asked_payload[:, 1:].reshape(width, 3, level_stack, PATCH, PATCH)

    valid = asked >= 0
    row0 = (asked // qy) * PATCH
    col0 = (asked % qy) * PATCH
    offs = jnp.arange(PATCH, dtype=jnp.int32)
    rows_at = jnp.arange(side_x, dtype=jnp.int32)
    cols_at = jnp.arange(side_y, dtype=jnp.int32)
    row_sel = (
        (rows_at[None, None, :] == (row0[:, None, None] + offs[None, :, None]))
        & valid[:, None, None]
    ).astype(jnp.float32)
    col_sel = (cols_at[None, None, :] == (col0[:, None, None] + offs[None, :, None])).astype(
        jnp.float32
    )
    picked_rows = jnp.einsum("kar,flrc->kflac", row_sel, tile, precision=HI)
    picked = jnp.einsum("kflac,kbc->kflab", picked_rows, col_sel, precision=HI)
    incoming = lax.all_to_all(
        picked.reshape(devices_y, capacity, cells), "gy", split_axis=0, concat_axis=0,
        tiled=True,
    ).reshape(width, cells)

    parent = jnp.take(incoming, slot_of, axis=0)
    coarse = parent.reshape(slots * 3 * level_stack, coarse_cells)
    upsampled = jnp.dot(coarse, spread, precision=HI)
    blended = smoothed + ALPHA * (upsampled - smoothed)

    codes = edge_rotation[0]
    flags = [
        my_column == 0,
        my_column == lax.axis_size("gx") - 1,
        my_row == 0,
        my_row == devices_y - 1,
    ]
    turns = edge_turns(codes, flags)
    fields = (tile[0], tile[1], tile[2])
    cell_coriolis = coriolis[0][None]
    for _ in range(NSUB):
        fields = substep(fields, cell_coriolis, turns, on_first_panel)

    block_mean = asked_means + ALPHA * (picked - asked_means)
    spread_cols = jnp.einsum("kflab,kbc->kflac", block_mean, col_sel, precision=HI)
    dense = jnp.einsum("kar,kflac->flrc", row_sel, spread_cols, precision=HI)
    row_mask = jnp.sum(row_sel, axis=1)
    col_mask = jnp.sum(col_sel, axis=1)
    count = jnp.dot(row_mask.T, col_mask, precision=HI)
    after = jnp.stack(fields, axis=0)
    final_result = after + BETA * (dense - count[None, None] * after)
    return (final_result[None], blended.reshape(1, 1, slots, 3, level_stack, fine_cells))


def solution(mesh):
    in_specs = (
        P("panel", None, None, "gx", "gy"),
        P("panel", "gx", "gy"),
        P("panel", None),
        P("panel", "gx", "gy", None, None, None),
        P("panel", "gx", "gy", None),
        P("panel", "gx", "gy"),
    )
    out_specs = (P("panel", None, None, "gx", "gy"), P("panel", "gx", "gy", None, None, None))
    return jax.shard_map(step, mesh=mesh, in_specs=in_specs, out_specs=out_specs, check_vma=False)
```

```python
import jax
import jax.numpy as jnp
from jax import lax
from jax.sharding import PartitionSpec as P

NSUB = 2
PATCH = 8
RATIO = 3
FINE = 24


DT_STEP = 0.25
GRAVITY = 1.0
DAMPING = 0.5
DEPTH = 1.0
KAPPA = 0.2
ALPHA = 0.5
BETA = 0.5

HI = lax.Precision.HIGHEST


def shift_pairs(count, step):
    return [(i, i + step) for i in range(count) if 0 <= i + step < count]


def centre(field):
    return field[..., 1:-1, 1:-1]


def along_x(field):
    return 0.5 * (field[..., 2:, 1:-1] - field[..., :-2, 1:-1])


def along_y(field):
    return 0.5 * (field[..., 1:-1, 2:] - field[..., 1:-1, :-2])


def laplacian(field):
    return (
        field[..., 2:, 1:-1]
        + field[..., :-2, 1:-1]
        + field[..., 1:-1, 2:]
        + field[..., 1:-1, :-2]
        - 4.0 * centre(field)
    )


def advance(height, east, north, coriolis):
    absolute = coriolis + along_x(north) - along_y(east)
    depth = DEPTH + height
    divergence = along_x(depth * east) + along_y(depth * north)
    new_height = centre(height) - DT_STEP * divergence
    new_east = centre(east) + DT_STEP * (
        absolute * centre(north) - GRAVITY * along_x(height) + DAMPING * laplacian(east)
    )
    new_north = centre(north) + DT_STEP * (
        -absolute * centre(east) - GRAVITY * along_y(height) + DAMPING * laplacian(north)
    )
    return (new_height, new_east, new_north)


def padded_field(field, west, east, south, north):
    rows = jnp.concatenate([west[:, None, :], field, east[:, None, :]], axis=1)
    zero = jnp.zeros_like(south[:, :1])
    low = jnp.concatenate([zero, south, zero], axis=1)[:, :, None]
    high = jnp.concatenate([zero, north, zero], axis=1)[:, :, None]
    return jnp.concatenate([low, rows, high], axis=2)


def edge_turns(codes):
    along = (codes == 0).astype(jnp.float32) - (codes == 2).astype(jnp.float32)
    across = (codes == 3).astype(jnp.float32) - (codes == 1).astype(jnp.float32)
    one = jnp.ones_like(along)
    zero = jnp.zeros_like(along)
    return jnp.stack(
        [
            jnp.stack([one, zero, zero], axis=1),
            jnp.stack([zero, along, across], axis=1),
            jnp.stack([zero, -across, along], axis=1),
        ],
        axis=1,
    )


def substep(fields, coriolis, turns, flags):
    nx = lax.axis_size("gx")
    ny = lax.axis_size("gy")
    first_rows = jnp.stack([f[:, 0, :] for f in fields], axis=0)
    last_rows = jnp.stack([f[:, -1, :] for f in fields], axis=0)
    first_cols = jnp.stack([f[:, :, 0] for f in fields], axis=0)
    last_cols = jnp.stack([f[:, :, -1] for f in fields], axis=0)
    strips = jnp.stack([first_rows, last_rows, first_cols, last_cols], axis=0)
    partner = lax.ppermute(strips, "panel", [(0, 1), (1, 0)])
    from_west = lax.ppermute(last_rows, "gx", shift_pairs(nx, 1))
    from_east = lax.ppermute(first_rows, "gx", shift_pairs(nx, -1))
    from_south = lax.ppermute(last_cols, "gy", shift_pairs(ny, 1))
    from_north = lax.ppermute(first_cols, "gy", shift_pairs(ny, -1))
    turned = jnp.einsum("sij,sjlc->silc", turns, partner, precision=HI)
    halos = [
        jnp.where(flags[side], turned[side], neighbour)
        for side, neighbour in enumerate((from_west, from_east, from_south, from_north))
    ]
    padded = [padded_field(fields[c], *(h[c] for h in halos)) for c in range(3)]
    return advance(padded[0], padded[1], padded[2], coriolis)


def step(state, coriolis, edge_rotation, nest_block_state, parent_tile_index, parent_spot_index):
    devices_y = lax.axis_size("gy")
    slots = nest_block_state.shape[2]
    capacity = 2
    width = devices_y * capacity
    my_row = lax.axis_index("gy")
    my_column = lax.axis_index("gx")
    tile = state[0]
    level_stack = tile.shape[1]
    side_x = tile.shape[2]
    side_y = tile.shape[3]
    qy = side_y // PATCH
    cells = 3 * level_stack * PATCH * PATCH
    fine_cells = FINE * FINE
    coarse_cells = PATCH * PATCH

    n_idx = jnp.arange(fine_cells, dtype=jnp.int32)
    fi = n_idx // FINE
    fj = n_idx % FINE
    coarse_of = (fi // RATIO) * PATCH + (fj // RATIO)
    m_idx = jnp.arange(coarse_cells, dtype=jnp.int32)
    spread = (m_idx[:, None] == coarse_of[None, :]).astype(jnp.float32)
    blocks = nest_block_state[0, 0].reshape(slots * 3 * level_stack, fine_cells)
    pad_lo = jnp.concatenate([blocks[:, :FINE], blocks[:, :-FINE]], axis=1)
    pad_hi = jnp.concatenate([blocks[:, FINE:], blocks[:, -FINE:]], axis=1)
    left = jnp.concatenate([blocks[:, :1], blocks[:, :-1]], axis=1)
    right = jnp.concatenate([blocks[:, 1:], blocks[:, -1:]], axis=1)
    left = jnp.where((fj == 0)[None, :], blocks, left)
    right = jnp.where((fj == FINE - 1)[None, :], blocks, right)
    lap = pad_hi + pad_lo + right + left - 4.0 * blocks
    smoothed = blocks + KAPPA * lap
    smooth_means = (jnp.dot(smoothed, spread.T, precision=HI) / float(RATIO * RATIO)).reshape(
        slots, cells
    )

    mine = parent_tile_index.reshape(slots)
    spots = parent_spot_index.reshape(slots)
    local = jnp.arange(slots, dtype=jnp.int32)
    rank = jnp.sum(
        ((mine[:, None] == mine[None, :]) & (local[None, :] < local[:, None])).astype(jnp.int32),
        axis=1,
    )
    slot_of = mine * capacity + rank
    slot_hit = (jnp.arange(width, dtype=jnp.int32)[:, None] == slot_of[None, :]).astype(
        jnp.float32
    )
    payload = jnp.concatenate(
        [(spots + 1).astype(jnp.float32)[:, None], smooth_means], axis=1
    )
    outgoing = jnp.dot(slot_hit, payload, precision=HI)
    asked_payload = lax.all_to_all(
        outgoing.reshape(devices_y, capacity, cells + 1), "gy", split_axis=0, concat_axis=0,
        tiled=True,
    ).reshape(width, cells + 1)
    asked = asked_payload[:, 0].astype(jnp.int32) - 1
    asked_means = asked_payload[:, 1:].reshape(width, 3, level_stack, PATCH, PATCH)

    valid = asked >= 0
    row0 = (asked // qy) * PATCH
    col0 = (asked % qy) * PATCH
    offs = jnp.arange(PATCH, dtype=jnp.int32)
    rows_at = jnp.arange(side_x, dtype=jnp.int32)
    cols_at = jnp.arange(side_y, dtype=jnp.int32)
    row_sel = (
        (rows_at[None, None, :] == (row0[:, None, None] + offs[None, :, None]))
        & valid[:, None, None]
    ).astype(jnp.float32)
    col_sel = (cols_at[None, None, :] == (col0[:, None, None] + offs[None, :, None])).astype(
        jnp.float32
    )
    picked_rows = jnp.einsum("kar,flrc->kflac", row_sel, tile, precision=HI)
    picked = jnp.einsum("kflac,kbc->kflab", picked_rows, col_sel, precision=HI)
    incoming = lax.all_to_all(
        picked.reshape(devices_y, capacity, cells), "gy", split_axis=0, concat_axis=0,
        tiled=True,
    ).reshape(width, cells)

    parent = jnp.take(incoming, slot_of, axis=0)
    coarse = parent.reshape(slots * 3 * level_stack, coarse_cells)
    upsampled = jnp.dot(coarse, spread, precision=HI)
    blended = smoothed + ALPHA * (upsampled - smoothed)

    codes = edge_rotation[0]
    flags = [
        my_column == 0,
        my_column == lax.axis_size("gx") - 1,
        my_row == 0,
        my_row == devices_y - 1,
    ]
    turns = edge_turns(codes)
    fields = (tile[0], tile[1], tile[2])
    cell_coriolis = coriolis[0][None]
    for _ in range(NSUB):
        fields = substep(fields, cell_coriolis, turns, flags)

    block_mean = asked_means + ALPHA * (picked - asked_means)
    spread_cols = jnp.einsum("kflab,kbc->kflac", block_mean, col_sel, precision=HI)
    dense = jnp.einsum("kar,kflac->flrc", row_sel, spread_cols, precision=HI)
    row_mask = jnp.sum(row_sel, axis=1)
    col_mask = jnp.sum(col_sel, axis=1)
    count = jnp.dot(row_mask.T, col_mask, precision=HI)
    after = jnp.stack(fields, axis=0)
    final_result = after + BETA * (dense - count[None, None] * after)
    return (final_result[None], blended.reshape(1, 1, slots, 3, level_stack, fine_cells))


def solution(mesh):
    in_specs = (
        P("panel", None, None, "gx", "gy"),
        P("panel", "gx", "gy"),
        P("panel", None),
        P("panel", "gx", "gy", None, None, None),
        P("panel", "gx", "gy", None),
        P("panel", "gx", "gy"),
    )
    out_specs = (P("panel", None, None, "gx", "gy"), P("panel", "gx", "gy", None, None, None))
    return jax.shard_map(step, mesh=mesh, in_specs=in_specs, out_specs=out_specs, check_vma=False)
```

```python
import jax
import jax.numpy as jnp
from jax import lax
from jax.sharding import PartitionSpec as P

PATCH = 8
RATIO = 3
FINE = 24


DT_STEP = 0.25
GRAVITY = 1.0
DAMPING = 0.5
DEPTH = 1.0
KAPPA = 0.2
ALPHA = 0.5
BETA = 0.5

HI = lax.Precision.HIGHEST


def shift_pairs(count, step):
    return [(i, i + step) for i in range(count) if 0 <= i + step < count]


def centre(field):
    return field[..., 1:-1, 1:-1]


def along_x(field):
    return 0.5 * (field[..., 2:, 1:-1] - field[..., :-2, 1:-1])


def along_y(field):
    return 0.5 * (field[..., 1:-1, 2:] - field[..., 1:-1, :-2])


def laplacian(field):
    return (
        field[..., 2:, 1:-1]
        + field[..., :-2, 1:-1]
        + field[..., 1:-1, 2:]
        + field[..., 1:-1, :-2]
        - 4.0 * centre(field)
    )


def advance(height, east, north, coriolis):
    absolute = coriolis + along_x(north) - along_y(east)
    depth = DEPTH + height
    divergence = along_x(depth * east) + along_y(depth * north)
    new_height = centre(height) - DT_STEP * divergence
    new_east = centre(east) + DT_STEP * (
        absolute * centre(north) - GRAVITY * along_x(height) + DAMPING * laplacian(east)
    )
    new_north = centre(north) + DT_STEP * (
        -absolute * centre(east) - GRAVITY * along_y(height) + DAMPING * laplacian(north)
    )
    return (new_height, new_east, new_north)


def padded_field(field, west, east, south, north):
    rows = jnp.concatenate([west[:, None, :], field, east[:, None, :]], axis=1)
    zero = jnp.zeros_like(south[:, :1])
    low = jnp.concatenate([zero, south, zero], axis=1)[:, :, None]
    high = jnp.concatenate([zero, north, zero], axis=1)[:, :, None]
    return jnp.concatenate([low, rows, high], axis=2)


def edge_turns(codes):
    along = (codes == 0).astype(jnp.float32) - (codes == 2).astype(jnp.float32)
    across = (codes == 3).astype(jnp.float32) - (codes == 1).astype(jnp.float32)
    one = jnp.ones_like(along)
    zero = jnp.zeros_like(along)
    return jnp.stack(
        [
            jnp.stack([one, zero, zero], axis=1),
            jnp.stack([zero, along, across], axis=1),
            jnp.stack([zero, -across, along], axis=1),
        ],
        axis=1,
    )


def edge_strips(fields):
    first_rows = jnp.stack([f[:, 0, :] for f in fields], axis=0)
    last_rows = jnp.stack([f[:, -1, :] for f in fields], axis=0)
    first_cols = jnp.stack([f[:, :, 0] for f in fields], axis=0)
    last_cols = jnp.stack([f[:, :, -1] for f in fields], axis=0)
    return first_rows, last_rows, first_cols, last_cols


def column_halos(first_cols, last_cols):
    count = lax.axis_size("gy")
    here = lax.axis_index("gy")
    target = jnp.arange(count, dtype=jnp.int32)
    to_next = (target == here + 1)[:, None, None, None]
    to_prev = (target == here - 1)[:, None, None, None]
    return jnp.where(to_next, last_cols[None], jnp.where(to_prev, first_cols[None], 0.0))


def received_columns(got):
    count = lax.axis_size("gy")
    here = lax.axis_index("gy")
    south = lax.dynamic_index_in_dim(got, jnp.maximum(here - 1, 0), axis=0, keepdims=False)
    north = lax.dynamic_index_in_dim(got, jnp.minimum(here + 1, count - 1), axis=0, keepdims=False)
    return south, north


def substep(fields, strips, from_south, from_north, coriolis, turns, flags):
    nx = lax.axis_size("gx")
    first_rows, last_rows, first_cols, last_cols = strips
    edges = jnp.stack([first_rows, last_rows, first_cols, last_cols], axis=0)
    partner = lax.ppermute(edges, "panel", [(0, 1), (1, 0)])
    from_west = lax.ppermute(last_rows, "gx", shift_pairs(nx, 1))
    from_east = lax.ppermute(first_rows, "gx", shift_pairs(nx, -1))
    turned = jnp.einsum("sij,sjlc->silc", turns, partner, precision=HI)
    halos = [
        jnp.where(flags[side], turned[side], neighbour)
        for side, neighbour in enumerate((from_west, from_east, from_south, from_north))
    ]
    padded = [padded_field(fields[c], *(h[c] for h in halos)) for c in range(3)]
    return advance(padded[0], padded[1], padded[2], coriolis)


def step(state, coriolis, edge_rotation, nest_block_state, parent_tile_index, parent_spot_index):
    devices_y = lax.axis_size("gy")
    slots = nest_block_state.shape[2]
    capacity = 2
    width = devices_y * capacity
    my_row = lax.axis_index("gy")
    my_column = lax.axis_index("gx")
    tile = state[0]
    level_stack = tile.shape[1]
    side_x = tile.shape[2]
    side_y = tile.shape[3]
    qy = side_y // PATCH
    cells = 3 * level_stack * PATCH * PATCH
    fine_cells = FINE * FINE
    coarse_cells = PATCH * PATCH

    n_idx = jnp.arange(fine_cells, dtype=jnp.int32)
    fi = n_idx // FINE
    fj = n_idx % FINE
    coarse_of = (fi // RATIO) * PATCH + (fj // RATIO)
    m_idx = jnp.arange(coarse_cells, dtype=jnp.int32)
    spread = (m_idx[:, None] == coarse_of[None, :]).astype(jnp.float32)
    blocks = nest_block_state[0, 0].reshape(slots * 3 * level_stack, fine_cells)
    pad_lo = jnp.concatenate([blocks[:, :FINE], blocks[:, :-FINE]], axis=1)
    pad_hi = jnp.concatenate([blocks[:, FINE:], blocks[:, -FINE:]], axis=1)
    left = jnp.concatenate([blocks[:, :1], blocks[:, :-1]], axis=1)
    right = jnp.concatenate([blocks[:, 1:], blocks[:, -1:]], axis=1)
    left = jnp.where((fj == 0)[None, :], blocks, left)
    right = jnp.where((fj == FINE - 1)[None, :], blocks, right)
    lap = pad_hi + pad_lo + right + left - 4.0 * blocks
    smoothed = blocks + KAPPA * lap
    smooth_means = (jnp.dot(smoothed, spread.T, precision=HI) / float(RATIO * RATIO)).reshape(
        slots, cells
    )

    mine = parent_tile_index.reshape(slots)
    spots = parent_spot_index.reshape(slots)
    local = jnp.arange(slots, dtype=jnp.int32)
    rank = jnp.sum(
        ((mine[:, None] == mine[None, :]) & (local[None, :] < local[:, None])).astype(jnp.int32),
        axis=1,
    )
    slot_of = mine * capacity + rank
    slot_hit = (jnp.arange(width, dtype=jnp.int32)[:, None] == slot_of[None, :]).astype(
        jnp.float32
    )
    payload = jnp.concatenate(
        [(spots + 1).astype(jnp.float32)[:, None], smooth_means], axis=1
    )
    outgoing = jnp.dot(slot_hit, payload, precision=HI)
    strips0 = edge_strips((tile[0], tile[1], tile[2]))
    columns0 = column_halos(strips0[2], strips0[3])
    ask_out = jnp.concatenate(
        [outgoing.reshape(devices_y, capacity * (cells + 1)), columns0.reshape(devices_y, -1)],
        axis=1,
    )
    ask_in = lax.all_to_all(ask_out, "gy", split_axis=0, concat_axis=0, tiled=True)
    asked_payload = ask_in[:, : capacity * (cells + 1)].reshape(width, cells + 1)
    got0 = ask_in[:, capacity * (cells + 1) :].reshape(columns0.shape)
    asked = asked_payload[:, 0].astype(jnp.int32) - 1
    asked_means = asked_payload[:, 1:].reshape(width, 3, level_stack, PATCH, PATCH)

    valid = asked >= 0
    row0 = (asked // qy) * PATCH
    col0 = (asked % qy) * PATCH
    offs = jnp.arange(PATCH, dtype=jnp.int32)
    rows_at = jnp.arange(side_x, dtype=jnp.int32)
    cols_at = jnp.arange(side_y, dtype=jnp.int32)
    row_sel = (
        (rows_at[None, None, :] == (row0[:, None, None] + offs[None, :, None]))
        & valid[:, None, None]
    ).astype(jnp.float32)
    col_sel = (cols_at[None, None, :] == (col0[:, None, None] + offs[None, :, None])).astype(
        jnp.float32
    )
    picked_rows = jnp.einsum("kar,flrc->kflac", row_sel, tile, precision=HI)
    picked = jnp.einsum("kflac,kbc->kflab", picked_rows, col_sel, precision=HI)
    codes = edge_rotation[0]
    flags = [
        my_column == 0,
        my_column == lax.axis_size("gx") - 1,
        my_row == 0,
        my_row == devices_y - 1,
    ]
    turns = edge_turns(codes)
    cell_coriolis = coriolis[0][None]
    south0, north0 = received_columns(got0)
    fields = substep(
        (tile[0], tile[1], tile[2]), strips0, south0, north0, cell_coriolis, turns, flags
    )
    strips1 = edge_strips(fields)
    columns1 = column_halos(strips1[2], strips1[3])
    answer_out = jnp.concatenate(
        [picked.reshape(devices_y, capacity * cells), columns1.reshape(devices_y, -1)], axis=1
    )
    answer_in = lax.all_to_all(answer_out, "gy", split_axis=0, concat_axis=0, tiled=True)
    incoming = answer_in[:, : capacity * cells].reshape(width, cells)
    got1 = answer_in[:, capacity * cells :].reshape(columns1.shape)
    south1, north1 = received_columns(got1)
    fields = substep(fields, strips1, south1, north1, cell_coriolis, turns, flags)

    parent = jnp.take(incoming, slot_of, axis=0)
    coarse = parent.reshape(slots * 3 * level_stack, coarse_cells)
    upsampled = jnp.dot(coarse, spread, precision=HI)
    blended = smoothed + ALPHA * (upsampled - smoothed)

    block_mean = asked_means + ALPHA * (picked - asked_means)
    spread_cols = jnp.einsum("kflab,kbc->kflac", block_mean, col_sel, precision=HI)
    dense = jnp.einsum("kar,kflac->flrc", row_sel, spread_cols, precision=HI)
    row_mask = jnp.sum(row_sel, axis=1)
    col_mask = jnp.sum(col_sel, axis=1)
    count = jnp.dot(row_mask.T, col_mask, precision=HI)
    after = jnp.stack(fields, axis=0)
    final_result = after + BETA * (dense - count[None, None] * after)
    return (final_result[None], blended.reshape(1, 1, slots, 3, level_stack, fine_cells))


def solution(mesh):
    in_specs = (
        P("panel", None, None, "gx", "gy"),
        P("panel", "gx", "gy"),
        P("panel", None),
        P("panel", "gx", "gy", None, None, None),
        P("panel", "gx", "gy", None),
        P("panel", "gx", "gy"),
    )
    out_specs = (P("panel", None, None, "gx", "gy"), P("panel", "gx", "gy", None, None, None))
    return jax.shard_map(step, mesh=mesh, in_specs=in_specs, out_specs=out_specs, check_vma=False)
```

```python
import jax
import jax.numpy as jnp
from jax import lax
from jax.sharding import PartitionSpec as P

PATCH = 8
RATIO = 3
FINE = 24


DT_STEP = 0.25
GRAVITY = 1.0
DAMPING = 0.5
DEPTH = 1.0
KAPPA = 0.2
ALPHA = 0.5
BETA = 0.5

HI = lax.Precision.HIGHEST


def shift_pairs(count, step):
    return [(i, i + step) for i in range(count) if 0 <= i + step < count]


def centre(field):
    return field[..., 1:-1, 1:-1]


def along_x(field):
    return 0.5 * (field[..., 2:, 1:-1] - field[..., :-2, 1:-1])


def along_y(field):
    return 0.5 * (field[..., 1:-1, 2:] - field[..., 1:-1, :-2])


def laplacian(field):
    return (
        field[..., 2:, 1:-1]
        + field[..., :-2, 1:-1]
        + field[..., 1:-1, 2:]
        + field[..., 1:-1, :-2]
        - 4.0 * centre(field)
    )


def advance(height, east, north, coriolis):
    absolute = coriolis + along_x(north) - along_y(east)
    depth = DEPTH + height
    divergence = along_x(depth * east) + along_y(depth * north)
    new_height = centre(height) - DT_STEP * divergence
    new_east = centre(east) + DT_STEP * (
        absolute * centre(north) - GRAVITY * along_x(height) + DAMPING * laplacian(east)
    )
    new_north = centre(north) + DT_STEP * (
        -absolute * centre(east) - GRAVITY * along_y(height) + DAMPING * laplacian(north)
    )
    return (new_height, new_east, new_north)


def padded_field(field, west, east, south, north):
    rows = jnp.concatenate([west[:, None, :], field, east[:, None, :]], axis=1)
    zero = jnp.zeros_like(south[:, :1])
    low = jnp.concatenate([zero, south, zero], axis=1)[:, :, None]
    high = jnp.concatenate([zero, north, zero], axis=1)[:, :, None]
    return jnp.concatenate([low, rows, high], axis=2)


def edge_turns(codes):
    along = (codes == 0).astype(jnp.float32) - (codes == 2).astype(jnp.float32)
    across = (codes == 3).astype(jnp.float32) - (codes == 1).astype(jnp.float32)
    one = jnp.ones_like(along)
    zero = jnp.zeros_like(along)
    return jnp.stack(
        [
            jnp.stack([one, zero, zero], axis=1),
            jnp.stack([zero, along, across], axis=1),
            jnp.stack([zero, -across, along], axis=1),
        ],
        axis=1,
    )


def edge_strips(fields):
    first_rows = jnp.stack([f[:, 0, :] for f in fields], axis=0)
    last_rows = jnp.stack([f[:, -1, :] for f in fields], axis=0)
    first_cols = jnp.stack([f[:, :, 0] for f in fields], axis=0)
    last_cols = jnp.stack([f[:, :, -1] for f in fields], axis=0)
    return first_rows, last_rows, first_cols, last_cols


def exchange(nest_part, first_rows, last_rows, first_cols, last_cols):
    count = lax.axis_size("gy")
    here = lax.axis_index("gy")
    on_first_panel = lax.axis_index("panel") == 0
    target = jnp.arange(count, dtype=jnp.int32)
    to_next = (target == here + 1)[:, None, None, None]
    to_prev = (target == here - 1)[:, None, None, None]
    columns = jnp.where(to_next, last_cols[None], jnp.where(to_prev, first_cols[None], 0.0))
    mine = jnp.concatenate([nest_part, columns.reshape(count, -1)], axis=1)
    row_edge = jnp.where(lax.axis_index("gx") == 0, first_rows, last_rows)
    col_edge = jnp.where(here == 0, first_cols, last_cols)
    edge = jnp.concatenate([row_edge.reshape(-1), col_edge.reshape(-1)])
    edge = jnp.pad(edge, (0, mine.shape[1] - edge.shape[0]))
    other = jnp.where((target == here)[:, None], edge[None], 0.0)
    sent = jnp.where(
        on_first_panel,
        jnp.concatenate([mine, other], axis=0),
        jnp.concatenate([other, mine], axis=0),
    )
    got = lax.all_to_all(sent, ("panel", "gy"), split_axis=0, concat_axis=0, tiled=True)
    own_start = jnp.where(on_first_panel, 0, count)
    partner_at = jnp.where(on_first_panel, count, 0) + here
    from_panel = lax.dynamic_slice_in_dim(got, own_start, count, axis=0)
    from_partner = lax.dynamic_index_in_dim(got, partner_at, axis=0, keepdims=False)
    nest_in = from_panel[:, : nest_part.shape[1]]
    got_columns = from_panel[:, nest_part.shape[1] :].reshape(columns.shape)
    south = lax.dynamic_index_in_dim(got_columns, jnp.maximum(here - 1, 0), axis=0, keepdims=False)
    north = lax.dynamic_index_in_dim(
        got_columns, jnp.minimum(here + 1, count - 1), axis=0, keepdims=False
    )
    strip = first_rows.size
    partner_row = from_partner[:strip].reshape(first_rows.shape)
    partner_col = from_partner[strip : 2 * strip].reshape(first_cols.shape)
    return nest_in, south, north, partner_row, partner_col


def substep(fields, strips, halos_y, coriolis, turns, flags):
    nx = lax.axis_size("gx")
    first_rows, last_rows, _, _ = strips
    from_south, from_north, partner_row, partner_col = halos_y
    from_west = lax.ppermute(last_rows, "gx", shift_pairs(nx, 1))
    from_east = lax.ppermute(first_rows, "gx", shift_pairs(nx, -1))
    partner = jnp.stack([partner_row, partner_row, partner_col, partner_col], axis=0)
    turned = jnp.einsum("sij,sjlc->silc", turns, partner, precision=HI)
    halos = [
        jnp.where(flags[side], turned[side], neighbour)
        for side, neighbour in enumerate((from_west, from_east, from_south, from_north))
    ]
    padded = [padded_field(fields[c], *(h[c] for h in halos)) for c in range(3)]
    return advance(padded[0], padded[1], padded[2], coriolis)


def step(state, coriolis, edge_rotation, nest_block_state, parent_tile_index, parent_spot_index):
    devices_y = lax.axis_size("gy")
    slots = nest_block_state.shape[2]
    capacity = 2
    width = devices_y * capacity
    my_row = lax.axis_index("gy")
    my_column = lax.axis_index("gx")
    tile = state[0]
    level_stack = tile.shape[1]
    side_x = tile.shape[2]
    side_y = tile.shape[3]
    qy = side_y // PATCH
    cells = 3 * level_stack * PATCH * PATCH
    fine_cells = FINE * FINE
    coarse_cells = PATCH * PATCH

    n_idx = jnp.arange(fine_cells, dtype=jnp.int32)
    fi = n_idx // FINE
    fj = n_idx % FINE
    coarse_of = (fi // RATIO) * PATCH + (fj // RATIO)
    m_idx = jnp.arange(coarse_cells, dtype=jnp.int32)
    spread = (m_idx[:, None] == coarse_of[None, :]).astype(jnp.float32)
    blocks = nest_block_state[0, 0].reshape(slots * 3 * level_stack, fine_cells)
    pad_lo = jnp.concatenate([blocks[:, :FINE], blocks[:, :-FINE]], axis=1)
    pad_hi = jnp.concatenate([blocks[:, FINE:], blocks[:, -FINE:]], axis=1)
    left = jnp.concatenate([blocks[:, :1], blocks[:, :-1]], axis=1)
    right = jnp.concatenate([blocks[:, 1:], blocks[:, -1:]], axis=1)
    left = jnp.where((fj == 0)[None, :], blocks, left)
    right = jnp.where((fj == FINE - 1)[None, :], blocks, right)
    lap = pad_hi + pad_lo + right + left - 4.0 * blocks
    smoothed = blocks + KAPPA * lap
    smooth_means = (jnp.dot(smoothed, spread.T, precision=HI) / float(RATIO * RATIO)).reshape(
        slots, cells
    )

    mine = parent_tile_index.reshape(slots)
    spots = parent_spot_index.reshape(slots)
    local = jnp.arange(slots, dtype=jnp.int32)
    rank = jnp.sum(
        ((mine[:, None] == mine[None, :]) & (local[None, :] < local[:, None])).astype(jnp.int32),
        axis=1,
    )
    slot_of = mine * capacity + rank
    slot_hit = (jnp.arange(width, dtype=jnp.int32)[:, None] == slot_of[None, :]).astype(
        jnp.float32
    )
    payload = jnp.concatenate(
        [(spots + 1).astype(jnp.float32)[:, None], smooth_means], axis=1
    )
    outgoing = jnp.dot(slot_hit, payload, precision=HI)
    strips0 = edge_strips((tile[0], tile[1], tile[2]))
    ask_in, south0, north0, partner_row0, partner_col0 = exchange(
        outgoing.reshape(devices_y, capacity * (cells + 1)), *strips0
    )
    asked_payload = ask_in.reshape(width, cells + 1)
    asked = asked_payload[:, 0].astype(jnp.int32) - 1
    asked_means = asked_payload[:, 1:].reshape(width, 3, level_stack, PATCH, PATCH)

    valid = asked >= 0
    row0 = (asked // qy) * PATCH
    col0 = (asked % qy) * PATCH
    offs = jnp.arange(PATCH, dtype=jnp.int32)
    rows_at = jnp.arange(side_x, dtype=jnp.int32)
    cols_at = jnp.arange(side_y, dtype=jnp.int32)
    row_sel = (
        (rows_at[None, None, :] == (row0[:, None, None] + offs[None, :, None]))
        & valid[:, None, None]
    ).astype(jnp.float32)
    col_sel = (cols_at[None, None, :] == (col0[:, None, None] + offs[None, :, None])).astype(
        jnp.float32
    )
    picked_rows = jnp.einsum("kar,flrc->kflac", row_sel, tile, precision=HI)
    picked = jnp.einsum("kflac,kbc->kflab", picked_rows, col_sel, precision=HI)
    codes = edge_rotation[0]
    flags = [
        my_column == 0,
        my_column == lax.axis_size("gx") - 1,
        my_row == 0,
        my_row == devices_y - 1,
    ]
    turns = edge_turns(codes)
    cell_coriolis = coriolis[0][None]
    fields = substep(
        (tile[0], tile[1], tile[2]),
        strips0,
        (south0, north0, partner_row0, partner_col0),
        cell_coriolis,
        turns,
        flags,
    )
    strips1 = edge_strips(fields)
    answer_in, south1, north1, partner_row1, partner_col1 = exchange(
        picked.reshape(devices_y, capacity * cells), *strips1
    )
    incoming = answer_in.reshape(width, cells)
    fields = substep(
        fields, strips1, (south1, north1, partner_row1, partner_col1), cell_coriolis, turns,
        flags,
    )

    parent = jnp.take(incoming, slot_of, axis=0)
    coarse = parent.reshape(slots * 3 * level_stack, coarse_cells)
    upsampled = jnp.dot(coarse, spread, precision=HI)
    blended = smoothed + ALPHA * (upsampled - smoothed)

    block_mean = asked_means + ALPHA * (picked - asked_means)
    spread_cols = jnp.einsum("kflab,kbc->kflac", block_mean, col_sel, precision=HI)
    dense = jnp.einsum("kar,kflac->flrc", row_sel, spread_cols, precision=HI)
    row_mask = jnp.sum(row_sel, axis=1)
    col_mask = jnp.sum(col_sel, axis=1)
    count = jnp.dot(row_mask.T, col_mask, precision=HI)
    after = jnp.stack(fields, axis=0)
    final_result = after + BETA * (dense - count[None, None] * after)
    return (final_result[None], blended.reshape(1, 1, slots, 3, level_stack, fine_cells))


def solution(mesh):
    in_specs = (
        P("panel", None, None, "gx", "gy"),
        P("panel", "gx", "gy"),
        P("panel", None),
        P("panel", "gx", "gy", None, None, None),
        P("panel", "gx", "gy", None),
        P("panel", "gx", "gy"),
    )
    out_specs = (P("panel", None, None, "gx", "gy"), P("panel", "gx", "gy", None, None, None))
    return jax.shard_map(step, mesh=mesh, in_specs=in_specs, out_specs=out_specs, check_vma=False)
```

```python
import jax
import jax.numpy as jnp
from jax import lax
from jax.sharding import PartitionSpec as P

PATCH = 8
RATIO = 3
FINE = 24


DT_STEP = 0.25
GRAVITY = 1.0
DAMPING = 0.5
DEPTH = 1.0
KAPPA = 0.2
ALPHA = 0.5
BETA = 0.5

HI = lax.Precision.HIGHEST


def shift_pairs(count, step):
    return [(i, i + step) for i in range(count) if 0 <= i + step < count]


def centre(field):
    return field[..., 1:-1, 1:-1]


def along_x(field):
    return 0.5 * (field[..., 2:, 1:-1] - field[..., :-2, 1:-1])


def along_y(field):
    return 0.5 * (field[..., 1:-1, 2:] - field[..., 1:-1, :-2])


def laplacian(field):
    return (
        field[..., 2:, 1:-1]
        + field[..., :-2, 1:-1]
        + field[..., 1:-1, 2:]
        + field[..., 1:-1, :-2]
        - 4.0 * centre(field)
    )


def advance(height, east, north, coriolis):
    absolute = coriolis + along_x(north) - along_y(east)
    depth = DEPTH + height
    divergence = along_x(depth * east) + along_y(depth * north)
    new_height = centre(height) - DT_STEP * divergence
    new_east = centre(east) + DT_STEP * (
        absolute * centre(north) - GRAVITY * along_x(height) + DAMPING * laplacian(east)
    )
    new_north = centre(north) + DT_STEP * (
        -absolute * centre(east) - GRAVITY * along_y(height) + DAMPING * laplacian(north)
    )
    return (new_height, new_east, new_north)


def padded_field(field, west, east, south, north):
    rows = jnp.concatenate([west[:, None, :], field, east[:, None, :]], axis=1)
    zero = jnp.zeros_like(south[:, :1])
    low = jnp.concatenate([zero, south, zero], axis=1)[:, :, None]
    high = jnp.concatenate([zero, north, zero], axis=1)[:, :, None]
    return jnp.concatenate([low, rows, high], axis=2)


def edge_turns(codes):
    along = (codes == 0).astype(jnp.float32) - (codes == 2).astype(jnp.float32)
    across = (codes == 3).astype(jnp.float32) - (codes == 1).astype(jnp.float32)
    one = jnp.ones_like(along)
    zero = jnp.zeros_like(along)
    return jnp.stack(
        [
            jnp.stack([one, zero, zero], axis=1),
            jnp.stack([zero, along, across], axis=1),
            jnp.stack([zero, -across, along], axis=1),
        ],
        axis=1,
    )


def edge_strips(fields):
    first_rows = jnp.stack([f[:, 0, :] for f in fields], axis=0)
    last_rows = jnp.stack([f[:, -1, :] for f in fields], axis=0)
    first_cols = jnp.stack([f[:, :, 0] for f in fields], axis=0)
    last_cols = jnp.stack([f[:, :, -1] for f in fields], axis=0)
    return first_rows, last_rows, first_cols, last_cols


def column_halos(first_cols, last_cols):
    count = lax.axis_size("gy")
    here = lax.axis_index("gy")
    target = jnp.arange(count, dtype=jnp.int32)
    to_next = (target == here + 1)[:, None, None, None]
    to_prev = (target == here - 1)[:, None, None, None]
    return jnp.where(to_next, last_cols[None], jnp.where(to_prev, first_cols[None], 0.0))


def received_columns(got):
    count = lax.axis_size("gy")
    here = lax.axis_index("gy")
    south = lax.dynamic_index_in_dim(got, jnp.maximum(here - 1, 0), axis=0, keepdims=False)
    north = lax.dynamic_index_in_dim(got, jnp.minimum(here + 1, count - 1), axis=0, keepdims=False)
    return south, north


def substep(fields, strips, from_south, from_north, coriolis, turns, flags):
    nx = lax.axis_size("gx")
    first_rows, last_rows, first_cols, last_cols = strips
    edges = jnp.stack([first_rows, last_rows, first_cols, last_cols], axis=0)
    partner = lax.ppermute(edges, "panel", [(0, 1), (1, 0)])
    from_west = lax.ppermute(last_rows, "gx", shift_pairs(nx, 1))
    from_east = lax.ppermute(first_rows, "gx", shift_pairs(nx, -1))
    turned = jnp.einsum("sij,sjlc->silc", turns, partner, precision=HI)
    halos = [
        jnp.where(flags[side], turned[side], neighbour)
        for side, neighbour in enumerate((from_west, from_east, from_south, from_north))
    ]
    padded = [padded_field(fields[c], *(h[c] for h in halos)) for c in range(3)]
    return advance(padded[0], padded[1], padded[2], coriolis)


def step(state, coriolis, edge_rotation, nest_block_state, parent_tile_index, parent_spot_index):
    devices_y = lax.axis_size("gy")
    slots = nest_block_state.shape[2]
    capacity = 2
    width = devices_y * capacity
    my_row = lax.axis_index("gy")
    my_column = lax.axis_index("gx")
    tile = state[0]
    level_stack = tile.shape[1]
    side_x = tile.shape[2]
    side_y = tile.shape[3]
    qy = side_y // PATCH
    cells = 3 * level_stack * PATCH * PATCH
    fine_cells = FINE * FINE
    coarse_cells = PATCH * PATCH

    n_idx = jnp.arange(fine_cells, dtype=jnp.int32)
    fi = n_idx // FINE
    fj = n_idx % FINE
    coarse_of = (fi // RATIO) * PATCH + (fj // RATIO)
    m_idx = jnp.arange(coarse_cells, dtype=jnp.int32)
    spread = (m_idx[:, None] == coarse_of[None, :]).astype(jnp.float32)
    blocks = nest_block_state[0, 0].reshape(slots * 3 * level_stack, fine_cells)
    pad_lo = jnp.concatenate([blocks[:, :FINE], blocks[:, :-FINE]], axis=1)
    pad_hi = jnp.concatenate([blocks[:, FINE:], blocks[:, -FINE:]], axis=1)
    left = jnp.concatenate([blocks[:, :1], blocks[:, :-1]], axis=1)
    right = jnp.concatenate([blocks[:, 1:], blocks[:, -1:]], axis=1)
    left = jnp.where((fj == 0)[None, :], blocks, left)
    right = jnp.where((fj == FINE - 1)[None, :], blocks, right)
    lap = pad_hi + pad_lo + right + left - 4.0 * blocks
    smoothed = blocks + KAPPA * lap
    smooth_means = (jnp.dot(smoothed, spread.T, precision=HI) / float(RATIO * RATIO)).reshape(
        slots, cells
    )

    mine = parent_tile_index.reshape(slots)
    spots = parent_spot_index.reshape(slots)
    local = jnp.arange(slots, dtype=jnp.int32)
    rank = jnp.sum(
        ((mine[:, None] == mine[None, :]) & (local[None, :] < local[:, None])).astype(jnp.int32),
        axis=1,
    )
    slot_of = mine * capacity + rank
    slot_hit = (jnp.arange(width, dtype=jnp.int32)[:, None] == slot_of[None, :]).astype(
        jnp.float32
    )
    outgoing = jnp.dot(slot_hit, (spots + 1).astype(jnp.float32)[:, None], precision=HI)
    strips0 = edge_strips((tile[0], tile[1], tile[2]))
    columns0 = column_halos(strips0[2], strips0[3])
    ask_out = jnp.concatenate(
        [outgoing.reshape(devices_y, capacity), columns0.reshape(devices_y, -1)], axis=1
    )
    ask_in = lax.all_to_all(ask_out, "gy", split_axis=0, concat_axis=0, tiled=True)
    got0 = ask_in[:, capacity:].reshape(columns0.shape)
    asked = ask_in[:, :capacity].reshape(width).astype(jnp.int32) - 1

    valid = asked >= 0
    row0 = (asked // qy) * PATCH
    col0 = (asked % qy) * PATCH
    offs = jnp.arange(PATCH, dtype=jnp.int32)
    rows_at = jnp.arange(side_x, dtype=jnp.int32)
    cols_at = jnp.arange(side_y, dtype=jnp.int32)
    row_sel = (
        (rows_at[None, None, :] == (row0[:, None, None] + offs[None, :, None]))
        & valid[:, None, None]
    ).astype(jnp.float32)
    col_sel = (cols_at[None, None, :] == (col0[:, None, None] + offs[None, :, None])).astype(
        jnp.float32
    )
    picked_rows = jnp.einsum("kar,flrc->kflac", row_sel, tile, precision=HI)
    picked = jnp.einsum("kflac,kbc->kflab", picked_rows, col_sel, precision=HI)
    codes = edge_rotation[0]
    flags = [
        my_column == 0,
        my_column == lax.axis_size("gx") - 1,
        my_row == 0,
        my_row == devices_y - 1,
    ]
    turns = edge_turns(codes)
    cell_coriolis = coriolis[0][None]
    south0, north0 = received_columns(got0)
    fields = substep(
        (tile[0], tile[1], tile[2]), strips0, south0, north0, cell_coriolis, turns, flags
    )
    strips1 = edge_strips(fields)
    columns1 = column_halos(strips1[2], strips1[3])
    held_means = jnp.dot(slot_hit, smooth_means, precision=HI)
    answer_out = jnp.concatenate(
        [
            picked.reshape(devices_y, capacity * cells),
            held_means.reshape(devices_y, capacity * cells),
            columns1.reshape(devices_y, -1),
        ],
        axis=1,
    )
    answer_in = lax.all_to_all(answer_out, "gy", split_axis=0, concat_axis=0, tiled=True)
    incoming = answer_in[:, : capacity * cells].reshape(width, cells)
    asked_means = answer_in[:, capacity * cells : 2 * capacity * cells].reshape(
        width, 3, level_stack, PATCH, PATCH
    )
    got1 = answer_in[:, 2 * capacity * cells :].reshape(columns1.shape)
    south1, north1 = received_columns(got1)
    fields = substep(fields, strips1, south1, north1, cell_coriolis, turns, flags)

    parent = jnp.take(incoming, slot_of, axis=0)
    coarse = parent.reshape(slots * 3 * level_stack, coarse_cells)
    upsampled = jnp.dot(coarse, spread, precision=HI)
    blended = smoothed + ALPHA * (upsampled - smoothed)

    block_mean = asked_means + ALPHA * (picked - asked_means)
    spread_cols = jnp.einsum("kflab,kbc->kflac", block_mean, col_sel, precision=HI)
    dense = jnp.einsum("kar,kflac->flrc", row_sel, spread_cols, precision=HI)
    row_mask = jnp.sum(row_sel, axis=1)
    col_mask = jnp.sum(col_sel, axis=1)
    count = jnp.dot(row_mask.T, col_mask, precision=HI)
    after = jnp.stack(fields, axis=0)
    final_result = after + BETA * (dense - count[None, None] * after)
    return (final_result[None], blended.reshape(1, 1, slots, 3, level_stack, fine_cells))


def solution(mesh):
    in_specs = (
        P("panel", None, None, "gx", "gy"),
        P("panel", "gx", "gy"),
        P("panel", None),
        P("panel", "gx", "gy", None, None, None),
        P("panel", "gx", "gy", None),
        P("panel", "gx", "gy"),
    )
    out_specs = (P("panel", None, None, "gx", "gy"), P("panel", "gx", "gy", None, None, None))
    return jax.shard_map(step, mesh=mesh, in_specs=in_specs, out_specs=out_specs, check_vma=False)
```

```python
import jax
import jax.numpy as jnp
from jax import lax
from jax.sharding import PartitionSpec as P

PATCH = 8
RATIO = 3
FINE = 24


DT_STEP = 0.25
GRAVITY = 1.0
DAMPING = 0.5
DEPTH = 1.0
KAPPA = 0.2
ALPHA = 0.5
BETA = 0.5

HI = lax.Precision.HIGHEST


def shift_pairs(count, step):
    return [(i, i + step) for i in range(count) if 0 <= i + step < count]


def centre(field):
    return field[..., 1:-1, 1:-1]


def along_x(field):
    return 0.5 * (field[..., 2:, 1:-1] - field[..., :-2, 1:-1])


def along_y(field):
    return 0.5 * (field[..., 1:-1, 2:] - field[..., 1:-1, :-2])


def laplacian(field):
    return (
        field[..., 2:, 1:-1]
        + field[..., :-2, 1:-1]
        + field[..., 1:-1, 2:]
        + field[..., 1:-1, :-2]
        - 4.0 * centre(field)
    )


def advance(height, east, north, coriolis):
    absolute = coriolis + along_x(north) - along_y(east)
    depth = DEPTH + height
    divergence = along_x(depth * east) + along_y(depth * north)
    new_height = centre(height) - DT_STEP * divergence
    new_east = centre(east) + DT_STEP * (
        absolute * centre(north) - GRAVITY * along_x(height) + DAMPING * laplacian(east)
    )
    new_north = centre(north) + DT_STEP * (
        -absolute * centre(east) - GRAVITY * along_y(height) + DAMPING * laplacian(north)
    )
    return (new_height, new_east, new_north)


def padded_field(field, west, east, south, north):
    rows = jnp.concatenate([west[:, None, :], field, east[:, None, :]], axis=1)
    zero = jnp.zeros_like(south[:, :1])
    low = jnp.concatenate([zero, south, zero], axis=1)[:, :, None]
    high = jnp.concatenate([zero, north, zero], axis=1)[:, :, None]
    return jnp.concatenate([low, rows, high], axis=2)


def edge_turns(codes):
    along = (codes == 0).astype(jnp.float32) - (codes == 2).astype(jnp.float32)
    across = (codes == 3).astype(jnp.float32) - (codes == 1).astype(jnp.float32)
    one = jnp.ones_like(along)
    zero = jnp.zeros_like(along)
    return jnp.stack(
        [
            jnp.stack([one, zero, zero], axis=1),
            jnp.stack([zero, along, across], axis=1),
            jnp.stack([zero, -across, along], axis=1),
        ],
        axis=1,
    )


def edge_strips(fields):
    first_rows = jnp.stack([f[:, 0, :] for f in fields], axis=0)
    last_rows = jnp.stack([f[:, -1, :] for f in fields], axis=0)
    first_cols = jnp.stack([f[:, :, 0] for f in fields], axis=0)
    last_cols = jnp.stack([f[:, :, -1] for f in fields], axis=0)
    return first_rows, last_rows, first_cols, last_cols


def column_halos(first_cols, last_cols):
    count = lax.axis_size("gy")
    here = lax.axis_index("gy")
    target = jnp.arange(count, dtype=jnp.int32)
    to_next = (target == here + 1)[:, None, None, None]
    to_prev = (target == here - 1)[:, None, None, None]
    return jnp.where(to_next, last_cols[None], jnp.where(to_prev, first_cols[None], 0.0))


def received_columns(got):
    count = lax.axis_size("gy")
    here = lax.axis_index("gy")
    south = lax.dynamic_index_in_dim(got, jnp.maximum(here - 1, 0), axis=0, keepdims=False)
    north = lax.dynamic_index_in_dim(got, jnp.minimum(here + 1, count - 1), axis=0, keepdims=False)
    return south, north


def substep(fields, strips, from_south, from_north, coriolis, turns, flags):
    nx = lax.axis_size("gx")
    first_rows, last_rows, first_cols, last_cols = strips
    edges = jnp.stack([first_rows, last_rows, first_cols, last_cols], axis=0)
    partner = lax.ppermute(edges, "panel", [(0, 1), (1, 0)])
    from_west = lax.ppermute(last_rows, "gx", shift_pairs(nx, 1))
    from_east = lax.ppermute(first_rows, "gx", shift_pairs(nx, -1))
    turned = jnp.einsum("sij,sjlc->silc", turns, partner, precision=HI)
    halos = [
        jnp.where(flags[side], turned[side], neighbour)
        for side, neighbour in enumerate((from_west, from_east, from_south, from_north))
    ]
    padded = [padded_field(fields[c], *(h[c] for h in halos)) for c in range(3)]
    return advance(padded[0], padded[1], padded[2], coriolis)


def step(state, coriolis, edge_rotation, nest_block_state, parent_tile_index, parent_spot_index):
    devices_y = lax.axis_size("gy")
    slots = nest_block_state.shape[2]
    capacity = 2
    width = devices_y * capacity
    my_row = lax.axis_index("gy")
    my_column = lax.axis_index("gx")
    tile = state[0]
    level_stack = tile.shape[1]
    side_x = tile.shape[2]
    side_y = tile.shape[3]
    qy = side_y // PATCH
    cells = 3 * level_stack * PATCH * PATCH
    fine_cells = FINE * FINE
    coarse_cells = PATCH * PATCH

    n_idx = jnp.arange(fine_cells, dtype=jnp.int32)
    fi = n_idx // FINE
    fj = n_idx % FINE
    coarse_of = (fi // RATIO) * PATCH + (fj // RATIO)
    m_idx = jnp.arange(coarse_cells, dtype=jnp.int32)
    spread = (m_idx[:, None] == coarse_of[None, :]).astype(jnp.float32)
    blocks = nest_block_state[0, 0].reshape(slots * 3 * level_stack, fine_cells)
    pad_lo = jnp.concatenate([blocks[:, :FINE], blocks[:, :-FINE]], axis=1)
    pad_hi = jnp.concatenate([blocks[:, FINE:], blocks[:, -FINE:]], axis=1)
    left = jnp.concatenate([blocks[:, :1], blocks[:, :-1]], axis=1)
    right = jnp.concatenate([blocks[:, 1:], blocks[:, -1:]], axis=1)
    left = jnp.where((fj == 0)[None, :], blocks, left)
    right = jnp.where((fj == FINE - 1)[None, :], blocks, right)
    lap = pad_hi + pad_lo + right + left - 4.0 * blocks
    smoothed = blocks + KAPPA * lap
    smooth_means = (jnp.dot(smoothed, spread.T, precision=HI) / float(RATIO * RATIO)).reshape(
        slots, cells
    )

    mine = parent_tile_index.reshape(slots)
    spots = parent_spot_index.reshape(slots)
    local = jnp.arange(slots, dtype=jnp.int32)
    rank = jnp.sum(
        ((mine[:, None] == mine[None, :]) & (local[None, :] < local[:, None])).astype(jnp.int32),
        axis=1,
    )
    slot_of = mine * capacity + rank
    slot_hit = (jnp.arange(width, dtype=jnp.int32)[:, None] == slot_of[None, :]).astype(
        jnp.float32
    )
    outgoing = jnp.dot(slot_hit, (spots + 1).astype(jnp.float32)[:, None], precision=HI)
    strips0 = edge_strips((tile[0], tile[1], tile[2]))
    columns0 = column_halos(strips0[2], strips0[3])
    ask_out = jnp.concatenate(
        [outgoing.reshape(devices_y, 1, capacity), columns0.reshape(devices_y, 1, -1)], axis=2
    )
    ask_in = lax.all_to_all(ask_out, "gy", split_axis=0, concat_axis=0, tiled=True)
    got0 = ask_in[:, 0, capacity:].reshape(columns0.shape)
    asked = ask_in[:, 0, :capacity].reshape(width).astype(jnp.int32) - 1

    valid = asked >= 0
    row0 = (asked // qy) * PATCH
    col0 = (asked % qy) * PATCH
    offs = jnp.arange(PATCH, dtype=jnp.int32)
    rows_at = jnp.arange(side_x, dtype=jnp.int32)
    cols_at = jnp.arange(side_y, dtype=jnp.int32)
    row_sel = (
        (rows_at[None, None, :] == (row0[:, None, None] + offs[None, :, None]))
        & valid[:, None, None]
    ).astype(jnp.float32)
    col_sel = (cols_at[None, None, :] == (col0[:, None, None] + offs[None, :, None])).astype(
        jnp.float32
    )
    picked_rows = jnp.einsum("kar,flrc->kflac", row_sel, tile, precision=HI)
    picked = jnp.einsum("kflac,kbc->kflab", picked_rows, col_sel, precision=HI)
    codes = edge_rotation[0]
    flags = [
        my_column == 0,
        my_column == lax.axis_size("gx") - 1,
        my_row == 0,
        my_row == devices_y - 1,
    ]
    turns = edge_turns(codes)
    cell_coriolis = coriolis[0][None]
    south0, north0 = received_columns(got0)
    fields = substep(
        (tile[0], tile[1], tile[2]), strips0, south0, north0, cell_coriolis, turns, flags
    )
    strips1 = edge_strips(fields)
    columns1 = column_halos(strips1[2], strips1[3])
    held_means = jnp.dot(slot_hit, smooth_means, precision=HI)
    answer_out = jnp.concatenate(
        [
            picked.reshape(devices_y, 1, capacity * cells),
            held_means.reshape(devices_y, 1, capacity * cells),
            columns1.reshape(devices_y, 1, -1),
        ],
        axis=2,
    )
    answer_in = lax.all_to_all(answer_out, "gy", split_axis=0, concat_axis=0, tiled=True)
    incoming = answer_in[:, 0, : capacity * cells].reshape(width, cells)
    asked_means = answer_in[:, 0, capacity * cells : 2 * capacity * cells].reshape(
        width, 3, level_stack, PATCH, PATCH
    )
    got1 = answer_in[:, 0, 2 * capacity * cells :].reshape(columns1.shape)
    south1, north1 = received_columns(got1)
    fields = substep(fields, strips1, south1, north1, cell_coriolis, turns, flags)

    parent = jnp.take(incoming, slot_of, axis=0)
    coarse = parent.reshape(slots * 3 * level_stack, coarse_cells)
    upsampled = jnp.dot(coarse, spread, precision=HI)
    blended = smoothed + ALPHA * (upsampled - smoothed)

    block_mean = asked_means + ALPHA * (picked - asked_means)
    spread_cols = jnp.einsum("kflab,kbc->kflac", block_mean, col_sel, precision=HI)
    dense = jnp.einsum("kar,kflac->flrc", row_sel, spread_cols, precision=HI)
    row_mask = jnp.sum(row_sel, axis=1)
    col_mask = jnp.sum(col_sel, axis=1)
    count = jnp.dot(row_mask.T, col_mask, precision=HI)
    dense, count = lax.optimization_barrier((dense, count))
    after = jnp.stack(fields, axis=0)
    final_result = after + BETA * (dense - count[None, None] * after)
    return (final_result[None], blended.reshape(1, 1, slots, 3, level_stack, fine_cells))


def solution(mesh):
    in_specs = (
        P("panel", None, None, "gx", "gy"),
        P("panel", "gx", "gy"),
        P("panel", None),
        P("panel", "gx", "gy", None, None, None),
        P("panel", "gx", "gy", None),
        P("panel", "gx", "gy"),
    )
    out_specs = (P("panel", None, None, "gx", "gy"), P("panel", "gx", "gy", None, None, None))
    return jax.shard_map(step, mesh=mesh, in_specs=in_specs, out_specs=out_specs, check_vma=False)
```

```python
import jax
import jax.numpy as jnp
from jax import lax
from jax.sharding import PartitionSpec as P

PATCH = 8
RATIO = 3
FINE = 24


DT_STEP = 0.25
GRAVITY = 1.0
DAMPING = 0.5
DEPTH = 1.0
KAPPA = 0.2
ALPHA = 0.5
BETA = 0.5

HI = lax.Precision.HIGHEST


def shift_pairs(count, step):
    return [(i, i + step) for i in range(count) if 0 <= i + step < count]


def shifted(field, west, east, south, north):
    x_plus = jnp.concatenate([field[:, 1:, :], east[:, None, :]], axis=1)
    x_minus = jnp.concatenate([west[:, None, :], field[:, :-1, :]], axis=1)
    y_plus = jnp.concatenate([field[:, :, 1:], north[:, :, None]], axis=2)
    y_minus = jnp.concatenate([south[:, :, None], field[:, :, :-1]], axis=2)
    return x_plus, x_minus, y_plus, y_minus


def advance_shifted(fields, halos, coriolis):
    height, east, north = fields
    hxp, hxm, hyp, hym = shifted(height, *(h[0] for h in halos))
    uxp, uxm, uyp, uym = shifted(east, *(h[1] for h in halos))
    vxp, vxm, vyp, vym = shifted(north, *(h[2] for h in halos))
    absolute = coriolis + 0.5 * (vxp - vxm) - 0.5 * (uyp - uym)
    divergence = 0.5 * ((DEPTH + hxp) * uxp - (DEPTH + hxm) * uxm) + 0.5 * (
        (DEPTH + hyp) * vyp - (DEPTH + hym) * vym
    )
    new_height = height - DT_STEP * divergence
    new_east = east + DT_STEP * (
        absolute * north
        - GRAVITY * (0.5 * (hxp - hxm))
        + DAMPING * (uxp + uxm + uyp + uym - 4.0 * east)
    )
    new_north = north + DT_STEP * (
        -absolute * east
        - GRAVITY * (0.5 * (hyp - hym))
        + DAMPING * (vxp + vxm + vyp + vym - 4.0 * north)
    )
    return (new_height, new_east, new_north)


def edge_turns(codes):
    along = (codes == 0).astype(jnp.float32) - (codes == 2).astype(jnp.float32)
    across = (codes == 3).astype(jnp.float32) - (codes == 1).astype(jnp.float32)
    one = jnp.ones_like(along)
    zero = jnp.zeros_like(along)
    return jnp.stack(
        [
            jnp.stack([one, zero, zero], axis=1),
            jnp.stack([zero, along, across], axis=1),
            jnp.stack([zero, -across, along], axis=1),
        ],
        axis=1,
    )


def edge_strips(fields):
    first_rows = jnp.stack([f[:, 0, :] for f in fields], axis=0)
    last_rows = jnp.stack([f[:, -1, :] for f in fields], axis=0)
    first_cols = jnp.stack([f[:, :, 0] for f in fields], axis=0)
    last_cols = jnp.stack([f[:, :, -1] for f in fields], axis=0)
    return first_rows, last_rows, first_cols, last_cols


def column_halos(first_cols, last_cols):
    count = lax.axis_size("gy")
    here = lax.axis_index("gy")
    target = jnp.arange(count, dtype=jnp.int32)
    to_next = (target == here + 1)[:, None, None, None]
    to_prev = (target == here - 1)[:, None, None, None]
    return jnp.where(to_next, last_cols[None], jnp.where(to_prev, first_cols[None], 0.0))


def received_columns(got):
    count = lax.axis_size("gy")
    here = lax.axis_index("gy")
    south = lax.dynamic_index_in_dim(got, jnp.maximum(here - 1, 0), axis=0, keepdims=False)
    north = lax.dynamic_index_in_dim(got, jnp.minimum(here + 1, count - 1), axis=0, keepdims=False)
    return south, north


def substep(fields, strips, from_south, from_north, coriolis, turns, flags):
    nx = lax.axis_size("gx")
    first_rows, last_rows, first_cols, last_cols = strips
    edges = jnp.stack([first_rows, last_rows, first_cols, last_cols], axis=0)
    partner = lax.ppermute(edges, "panel", [(0, 1), (1, 0)])
    from_west = lax.ppermute(last_rows, "gx", shift_pairs(nx, 1))
    from_east = lax.ppermute(first_rows, "gx", shift_pairs(nx, -1))
    turned = jnp.einsum("sij,sjlc->silc", turns, partner, precision=HI)
    halos = [
        jnp.where(flags[side], turned[side], neighbour)
        for side, neighbour in enumerate((from_west, from_east, from_south, from_north))
    ]
    return advance_shifted(fields, halos, coriolis)


def step(state, coriolis, edge_rotation, nest_block_state, parent_tile_index, parent_spot_index):
    devices_y = lax.axis_size("gy")
    slots = nest_block_state.shape[2]
    capacity = 2
    width = devices_y * capacity
    my_row = lax.axis_index("gy")
    my_column = lax.axis_index("gx")
    tile = state[0]
    level_stack = tile.shape[1]
    side_x = tile.shape[2]
    side_y = tile.shape[3]
    qy = side_y // PATCH
    cells = 3 * level_stack * PATCH * PATCH
    fine_cells = FINE * FINE
    coarse_cells = PATCH * PATCH

    n_idx = jnp.arange(fine_cells, dtype=jnp.int32)
    fi = n_idx // FINE
    fj = n_idx % FINE
    coarse_of = (fi // RATIO) * PATCH + (fj // RATIO)
    m_idx = jnp.arange(coarse_cells, dtype=jnp.int32)
    spread = (m_idx[:, None] == coarse_of[None, :]).astype(jnp.float32)
    blocks = nest_block_state[0, 0].reshape(slots * 3 * level_stack, fine_cells)
    pad_lo = jnp.concatenate([blocks[:, :FINE], blocks[:, :-FINE]], axis=1)
    pad_hi = jnp.concatenate([blocks[:, FINE:], blocks[:, -FINE:]], axis=1)
    left = jnp.concatenate([blocks[:, :1], blocks[:, :-1]], axis=1)
    right = jnp.concatenate([blocks[:, 1:], blocks[:, -1:]], axis=1)
    left = jnp.where((fj == 0)[None, :], blocks, left)
    right = jnp.where((fj == FINE - 1)[None, :], blocks, right)
    lap = pad_hi + pad_lo + right + left - 4.0 * blocks
    smoothed = blocks + KAPPA * lap
    smooth_means = (jnp.dot(smoothed, spread.T, precision=HI) / float(RATIO * RATIO)).reshape(
        slots, cells
    )

    mine = parent_tile_index.reshape(slots)
    spots = parent_spot_index.reshape(slots)
    local = jnp.arange(slots, dtype=jnp.int32)
    rank = jnp.sum(
        ((mine[:, None] == mine[None, :]) & (local[None, :] < local[:, None])).astype(jnp.int32),
        axis=1,
    )
    slot_of = mine * capacity + rank
    slot_hit = (jnp.arange(width, dtype=jnp.int32)[:, None] == slot_of[None, :]).astype(
        jnp.float32
    )
    payload = jnp.concatenate(
        [(spots + 1).astype(jnp.float32)[:, None], smooth_means], axis=1
    )
    outgoing = jnp.dot(slot_hit, payload, precision=HI)
    strips0 = edge_strips((tile[0], tile[1], tile[2]))
    columns0 = column_halos(strips0[2], strips0[3])
    ask_out = jnp.concatenate(
        [
            outgoing.reshape(devices_y, 1, capacity * (cells + 1)),
            columns0.reshape(devices_y, 1, -1),
        ],
        axis=2,
    )
    ask_in = lax.all_to_all(ask_out, "gy", split_axis=0, concat_axis=0, tiled=True)
    asked_payload = ask_in[:, 0, : capacity * (cells + 1)].reshape(width, cells + 1)
    got0 = ask_in[:, 0, capacity * (cells + 1) :].reshape(columns0.shape)
    asked = asked_payload[:, 0].astype(jnp.int32) - 1
    asked_means = asked_payload[:, 1:].reshape(width, 3, level_stack, PATCH, PATCH)

    valid = asked >= 0
    row0 = (asked // qy) * PATCH
    col0 = (asked % qy) * PATCH
    offs = jnp.arange(PATCH, dtype=jnp.int32)
    rows_at = jnp.arange(side_x, dtype=jnp.int32)
    cols_at = jnp.arange(side_y, dtype=jnp.int32)
    row_sel = (
        (rows_at[None, None, :] == (row0[:, None, None] + offs[None, :, None]))
        & valid[:, None, None]
    ).astype(jnp.float32)
    col_sel = (cols_at[None, None, :] == (col0[:, None, None] + offs[None, :, None])).astype(
        jnp.float32
    )
    picked_rows = jnp.einsum("kar,flrc->kflac", row_sel, tile, precision=HI)
    picked = jnp.einsum("kflac,kbc->kflab", picked_rows, col_sel, precision=HI)
    codes = edge_rotation[0]
    flags = [
        my_column == 0,
        my_column == lax.axis_size("gx") - 1,
        my_row == 0,
        my_row == devices_y - 1,
    ]
    turns = edge_turns(codes)
    cell_coriolis = coriolis[0][None]
    south0, north0 = received_columns(got0)
    fields = substep(
        (tile[0], tile[1], tile[2]), strips0, south0, north0, cell_coriolis, turns, flags
    )
    strips1 = edge_strips(fields)
    columns1 = column_halos(strips1[2], strips1[3])
    answer_out = jnp.concatenate(
        [picked.reshape(devices_y, 1, capacity * cells), columns1.reshape(devices_y, 1, -1)],
        axis=2,
    )
    answer_in = lax.all_to_all(answer_out, "gy", split_axis=0, concat_axis=0, tiled=True)
    incoming = answer_in[:, 0, : capacity * cells].reshape(width, cells)
    got1 = answer_in[:, 0, capacity * cells :].reshape(columns1.shape)
    south1, north1 = received_columns(got1)
    fields = substep(fields, strips1, south1, north1, cell_coriolis, turns, flags)

    parent = jnp.take(incoming, slot_of, axis=0)
    coarse = parent.reshape(slots * 3 * level_stack, coarse_cells)
    upsampled = jnp.dot(coarse, spread, precision=HI)
    blended = smoothed + ALPHA * (upsampled - smoothed)

    block_mean = asked_means + ALPHA * (picked - asked_means)
    spread_cols = jnp.einsum("kflab,kbc->kflac", block_mean, col_sel, precision=HI)
    dense = jnp.einsum("kar,kflac->flrc", row_sel, spread_cols, precision=HI)
    row_mask = jnp.sum(row_sel, axis=1)
    col_mask = jnp.sum(col_sel, axis=1)
    count = jnp.dot(row_mask.T, col_mask, precision=HI)
    dense, count = lax.optimization_barrier((dense, count))
    after = jnp.stack(fields, axis=0)
    final_result = after + BETA * (dense - count[None, None] * after)
    return (final_result[None], blended.reshape(1, 1, slots, 3, level_stack, fine_cells))


def solution(mesh):
    in_specs = (
        P("panel", None, None, "gx", "gy"),
        P("panel", "gx", "gy"),
        P("panel", None),
        P("panel", "gx", "gy", None, None, None),
        P("panel", "gx", "gy", None),
        P("panel", "gx", "gy"),
    )
    out_specs = (P("panel", None, None, "gx", "gy"), P("panel", "gx", "gy", None, None, None))
    return jax.shard_map(step, mesh=mesh, in_specs=in_specs, out_specs=out_specs, check_vma=False)
```

```python
import jax
import jax.numpy as jnp
from jax import lax
from jax.sharding import PartitionSpec as P

PATCH = 8
RATIO = 3
FINE = 24


DT_STEP = 0.25
GRAVITY = 1.0
DAMPING = 0.5
DEPTH = 1.0
KAPPA = 0.2
ALPHA = 0.5
BETA = 0.5

HI = lax.Precision.HIGHEST


def shift_pairs(count, step):
    return [(i, i + step) for i in range(count) if 0 <= i + step < count]


def centre(field):
    return field[..., 1:-1, 1:-1]


def along_x(field):
    return 0.5 * (field[..., 2:, 1:-1] - field[..., :-2, 1:-1])


def along_y(field):
    return 0.5 * (field[..., 1:-1, 2:] - field[..., 1:-1, :-2])


def laplacian(field):
    return (
        field[..., 2:, 1:-1]
        + field[..., :-2, 1:-1]
        + field[..., 1:-1, 2:]
        + field[..., 1:-1, :-2]
        - 4.0 * centre(field)
    )


def advance(height, east, north, coriolis):
    absolute = coriolis + along_x(north) - along_y(east)
    depth = DEPTH + height
    divergence = along_x(depth * east) + along_y(depth * north)
    new_height = centre(height) - DT_STEP * divergence
    new_east = centre(east) + DT_STEP * (
        absolute * centre(north) - GRAVITY * along_x(height) + DAMPING * laplacian(east)
    )
    new_north = centre(north) + DT_STEP * (
        -absolute * centre(east) - GRAVITY * along_y(height) + DAMPING * laplacian(north)
    )
    return (new_height, new_east, new_north)


def padded_field(field, west, east, south, north):
    rows = jnp.concatenate([west[:, None, :], field, east[:, None, :]], axis=1)
    zero = jnp.zeros_like(south[:, :1])
    low = jnp.concatenate([zero, south, zero], axis=1)[:, :, None]
    high = jnp.concatenate([zero, north, zero], axis=1)[:, :, None]
    return jnp.concatenate([low, rows, high], axis=2)


def edge_turns(codes):
    along = (codes == 0).astype(jnp.float32) - (codes == 2).astype(jnp.float32)
    across = (codes == 3).astype(jnp.float32) - (codes == 1).astype(jnp.float32)
    one = jnp.ones_like(along)
    zero = jnp.zeros_like(along)
    return jnp.stack(
        [
            jnp.stack([one, zero, zero], axis=1),
            jnp.stack([zero, along, across], axis=1),
            jnp.stack([zero, -across, along], axis=1),
        ],
        axis=1,
    )


def edge_strips(fields):
    first_rows = jnp.stack([f[:, 0, :] for f in fields], axis=0)
    last_rows = jnp.stack([f[:, -1, :] for f in fields], axis=0)
    first_cols = jnp.stack([f[:, :, 0] for f in fields], axis=0)
    last_cols = jnp.stack([f[:, :, -1] for f in fields], axis=0)
    return first_rows, last_rows, first_cols, last_cols


def column_halos(first_cols, last_cols):
    count = lax.axis_size("gy")
    here = lax.axis_index("gy")
    target = jnp.arange(count, dtype=jnp.int32)
    to_next = (target == here + 1)[:, None, None, None]
    to_prev = (target == here - 1)[:, None, None, None]
    return jnp.where(to_next, last_cols[None], jnp.where(to_prev, first_cols[None], 0.0))


def received_columns(got):
    count = lax.axis_size("gy")
    here = lax.axis_index("gy")
    south = lax.dynamic_index_in_dim(got, jnp.maximum(here - 1, 0), axis=0, keepdims=False)
    north = lax.dynamic_index_in_dim(got, jnp.minimum(here + 1, count - 1), axis=0, keepdims=False)
    return south, north


def substep(fields, strips, from_south, from_north, coriolis, turns, flags):
    nx = lax.axis_size("gx")
    first_rows, last_rows, first_cols, last_cols = strips
    edges = jnp.stack([first_rows, last_rows, first_cols, last_cols], axis=0)
    partner = lax.ppermute(edges, "panel", [(0, 1), (1, 0)])
    from_west = lax.ppermute(last_rows, "gx", shift_pairs(nx, 1))
    from_east = lax.ppermute(first_rows, "gx", shift_pairs(nx, -1))
    turned = jnp.einsum("sij,sjlc->silc", turns, partner, precision=HI)
    halos = [
        jnp.where(flags[side], turned[side], neighbour)
        for side, neighbour in enumerate((from_west, from_east, from_south, from_north))
    ]
    padded = [padded_field(fields[c], *(h[c] for h in halos)) for c in range(3)]
    return advance(padded[0], padded[1], padded[2], coriolis)


def step(state, coriolis, edge_rotation, nest_block_state, parent_tile_index, parent_spot_index):
    devices_y = lax.axis_size("gy")
    slots = nest_block_state.shape[2]
    capacity = 2
    width = devices_y * capacity
    my_row = lax.axis_index("gy")
    my_column = lax.axis_index("gx")
    tile = state[0]
    level_stack = tile.shape[1]
    side_x = tile.shape[2]
    side_y = tile.shape[3]
    qy = side_y // PATCH
    cells = 3 * level_stack * PATCH * PATCH
    fine_cells = FINE * FINE
    coarse_cells = PATCH * PATCH

    n_idx = jnp.arange(fine_cells, dtype=jnp.int32)
    fi = n_idx // FINE
    fj = n_idx % FINE
    coarse_of = (fi // RATIO) * PATCH + (fj // RATIO)
    m_idx = jnp.arange(coarse_cells, dtype=jnp.int32)
    spread = (m_idx[:, None] == coarse_of[None, :]).astype(jnp.float32)
    blocks = nest_block_state[0, 0]
    pad_lo = jnp.concatenate([blocks[..., :FINE], blocks[..., :-FINE]], axis=-1)
    pad_hi = jnp.concatenate([blocks[..., FINE:], blocks[..., -FINE:]], axis=-1)
    left = jnp.concatenate([blocks[..., :1], blocks[..., :-1]], axis=-1)
    right = jnp.concatenate([blocks[..., 1:], blocks[..., -1:]], axis=-1)
    left = jnp.where(fj == 0, blocks, left)
    right = jnp.where(fj == FINE - 1, blocks, right)
    lap = pad_hi + pad_lo + right + left - 4.0 * blocks
    smoothed = blocks + KAPPA * lap
    smooth_means = (
        jnp.einsum("bfln,mn->bflm", smoothed, spread, precision=HI) / float(RATIO * RATIO)
    ).reshape(slots, cells)

    mine = parent_tile_index.reshape(slots)
    spots = parent_spot_index.reshape(slots)
    local = jnp.arange(slots, dtype=jnp.int32)
    rank = jnp.sum(
        ((mine[:, None] == mine[None, :]) & (local[None, :] < local[:, None])).astype(jnp.int32),
        axis=1,
    )
    slot_of = mine * capacity + rank
    slot_hit = (jnp.arange(width, dtype=jnp.int32)[:, None] == slot_of[None, :]).astype(
        jnp.float32
    )
    payload = jnp.concatenate(
        [(spots + 1).astype(jnp.float32)[:, None], smooth_means], axis=1
    )
    outgoing = jnp.dot(slot_hit, payload, precision=HI)
    strips0 = edge_strips((tile[0], tile[1], tile[2]))
    columns0 = column_halos(strips0[2], strips0[3])
    ask_out = jnp.concatenate(
        [
            outgoing.reshape(devices_y, 1, capacity * (cells + 1)),
            columns0.reshape(devices_y, 1, -1),
        ],
        axis=2,
    )
    ask_in = lax.all_to_all(ask_out, "gy", split_axis=0, concat_axis=0, tiled=True)
    asked_payload = ask_in[:, 0, : capacity * (cells + 1)].reshape(width, cells + 1)
    got0 = ask_in[:, 0, capacity * (cells + 1) :].reshape(columns0.shape)
    asked = asked_payload[:, 0].astype(jnp.int32) - 1
    asked_means = asked_payload[:, 1:].reshape(width, 3, level_stack, PATCH, PATCH)

    valid = asked >= 0
    row0 = (asked // qy) * PATCH
    col0 = (asked % qy) * PATCH
    offs = jnp.arange(PATCH, dtype=jnp.int32)
    rows_at = jnp.arange(side_x, dtype=jnp.int32)
    cols_at = jnp.arange(side_y, dtype=jnp.int32)
    row_sel = (
        (rows_at[None, None, :] == (row0[:, None, None] + offs[None, :, None]))
        & valid[:, None, None]
    ).astype(jnp.float32)
    col_sel = (cols_at[None, None, :] == (col0[:, None, None] + offs[None, :, None])).astype(
        jnp.float32
    )
    picked_rows = jnp.einsum("kar,flrc->kflac", row_sel, tile, precision=HI)
    picked = jnp.einsum("kflac,kbc->kflab", picked_rows, col_sel, precision=HI)
    codes = edge_rotation[0]
    flags = [
        my_column == 0,
        my_column == lax.axis_size("gx") - 1,
        my_row == 0,
        my_row == devices_y - 1,
    ]
    turns = edge_turns(codes)
    cell_coriolis = coriolis[0][None]
    south0, north0 = received_columns(got0)
    fields = substep(
        (tile[0], tile[1], tile[2]), strips0, south0, north0, cell_coriolis, turns, flags
    )
    strips1 = edge_strips(fields)
    columns1 = column_halos(strips1[2], strips1[3])
    answer_out = jnp.concatenate(
        [picked.reshape(devices_y, 1, capacity * cells), columns1.reshape(devices_y, 1, -1)],
        axis=2,
    )
    answer_in = lax.all_to_all(answer_out, "gy", split_axis=0, concat_axis=0, tiled=True)
    incoming = answer_in[:, 0, : capacity * cells].reshape(width, cells)
    got1 = answer_in[:, 0, capacity * cells :].reshape(columns1.shape)
    south1, north1 = received_columns(got1)
    fields = substep(fields, strips1, south1, north1, cell_coriolis, turns, flags)

    parent = jnp.take(incoming, slot_of, axis=0)
    coarse = parent.reshape(slots, 3, level_stack, coarse_cells)
    upsampled = jnp.einsum("bflm,mn->bfln", coarse, spread, precision=HI)
    blended = smoothed + ALPHA * (upsampled - smoothed)

    block_mean = asked_means + ALPHA * (picked - asked_means)
    spread_cols = jnp.einsum("kflab,kbc->kflac", block_mean, col_sel, precision=HI)
    dense = jnp.einsum("kar,kflac->flrc", row_sel, spread_cols, precision=HI)
    row_mask = jnp.sum(row_sel, axis=1)
    col_mask = jnp.sum(col_sel, axis=1)
    count = jnp.dot(row_mask.T, col_mask, precision=HI)
    dense, count = lax.optimization_barrier((dense, count))
    after = jnp.stack(fields, axis=0)
    final_result = after + BETA * (dense - count[None, None] * after)
    return (final_result[None], blended.reshape(1, 1, slots, 3, level_stack, fine_cells))


def solution(mesh):
    in_specs = (
        P("panel", None, None, "gx", "gy"),
        P("panel", "gx", "gy"),
        P("panel", None),
        P("panel", "gx", "gy", None, None, None),
        P("panel", "gx", "gy", None),
        P("panel", "gx", "gy"),
    )
    out_specs = (P("panel", None, None, "gx", "gy"), P("panel", "gx", "gy", None, None, None))
    return jax.shard_map(step, mesh=mesh, in_specs=in_specs, out_specs=out_specs, check_vma=False)
```

```python
import jax
import jax.numpy as jnp
from jax import lax
from jax.sharding import PartitionSpec as P

PATCH = 8
RATIO = 3
FINE = 24


DT_STEP = 0.25
GRAVITY = 1.0
DAMPING = 0.5
DEPTH = 1.0
KAPPA = 0.2
ALPHA = 0.5
BETA = 0.5

HI = lax.Precision.HIGHEST


def shift_pairs(count, step):
    return [(i, i + step) for i in range(count) if 0 <= i + step < count]


def centre(field):
    return field[..., 1:-1, 1:-1]


def along_x(field):
    return 0.5 * (field[..., 2:, 1:-1] - field[..., :-2, 1:-1])


def along_y(field):
    return 0.5 * (field[..., 1:-1, 2:] - field[..., 1:-1, :-2])


def laplacian(field):
    return (
        field[..., 2:, 1:-1]
        + field[..., :-2, 1:-1]
        + field[..., 1:-1, 2:]
        + field[..., 1:-1, :-2]
        - 4.0 * centre(field)
    )


def advance(height, east, north, coriolis):
    absolute = coriolis + along_x(north) - along_y(east)
    depth = DEPTH + height
    divergence = along_x(depth * east) + along_y(depth * north)
    new_height = centre(height) - DT_STEP * divergence
    new_east = centre(east) + DT_STEP * (
        absolute * centre(north) - GRAVITY * along_x(height) + DAMPING * laplacian(east)
    )
    new_north = centre(north) + DT_STEP * (
        -absolute * centre(east) - GRAVITY * along_y(height) + DAMPING * laplacian(north)
    )
    return (new_height, new_east, new_north)


def padded_field(field, west, east, south, north):
    rows = jnp.concatenate([west[:, None, :], field, east[:, None, :]], axis=1)
    zero = jnp.zeros_like(south[:, :1])
    low = jnp.concatenate([zero, south, zero], axis=1)[:, :, None]
    high = jnp.concatenate([zero, north, zero], axis=1)[:, :, None]
    return jnp.concatenate([low, rows, high], axis=2)


def edge_turns(codes):
    along = (codes == 0).astype(jnp.float32) - (codes == 2).astype(jnp.float32)
    across = (codes == 3).astype(jnp.float32) - (codes == 1).astype(jnp.float32)
    one = jnp.ones_like(along)
    zero = jnp.zeros_like(along)
    return jnp.stack(
        [
            jnp.stack([one, zero, zero], axis=1),
            jnp.stack([zero, along, across], axis=1),
            jnp.stack([zero, -across, along], axis=1),
        ],
        axis=1,
    )


def edge_strips(fields):
    first_rows = jnp.stack([f[:, 0, :] for f in fields], axis=0)
    last_rows = jnp.stack([f[:, -1, :] for f in fields], axis=0)
    first_cols = jnp.stack([f[:, :, 0] for f in fields], axis=0)
    last_cols = jnp.stack([f[:, :, -1] for f in fields], axis=0)
    return first_rows, last_rows, first_cols, last_cols


def column_halos(first_cols, last_cols):
    count = lax.axis_size("gy")
    here = lax.axis_index("gy")
    target = jnp.arange(count, dtype=jnp.int32)
    to_next = (target == here + 1)[:, None, None, None]
    to_prev = (target == here - 1)[:, None, None, None]
    return jnp.where(to_next, last_cols[None], jnp.where(to_prev, first_cols[None], 0.0))


def received_columns(got):
    count = lax.axis_size("gy")
    here = lax.axis_index("gy")
    south = lax.dynamic_index_in_dim(got, jnp.maximum(here - 1, 0), axis=0, keepdims=False)
    north = lax.dynamic_index_in_dim(got, jnp.minimum(here + 1, count - 1), axis=0, keepdims=False)
    return south, north


def substep(fields, strips, from_south, from_north, coriolis, turns, flags):
    nx = lax.axis_size("gx")
    first_rows, last_rows, first_cols, last_cols = strips
    edges = jnp.stack([first_rows, last_rows, first_cols, last_cols], axis=0)
    partner = lax.ppermute(edges, "panel", [(0, 1), (1, 0)])
    from_west = lax.ppermute(last_rows, "gx", shift_pairs(nx, 1))
    from_east = lax.ppermute(first_rows, "gx", shift_pairs(nx, -1))
    turned = jnp.einsum("sij,sjlc->silc", turns, partner, precision=HI)
    halos = [
        jnp.where(flags[side], turned[side], neighbour)
        for side, neighbour in enumerate((from_west, from_east, from_south, from_north))
    ]
    padded = [padded_field(fields[c], *(h[c] for h in halos)) for c in range(3)]
    return advance(padded[0], padded[1], padded[2], coriolis)


def step(state, coriolis, edge_rotation, nest_block_state, parent_tile_index, parent_spot_index):
    devices_y = lax.axis_size("gy")
    slots = nest_block_state.shape[2]
    capacity = 2
    width = devices_y * capacity
    my_row = lax.axis_index("gy")
    my_column = lax.axis_index("gx")
    tile = state[0]
    level_stack = tile.shape[1]
    side_x = tile.shape[2]
    side_y = tile.shape[3]
    qy = side_y // PATCH
    cells = 3 * level_stack * PATCH * PATCH
    fine_cells = FINE * FINE
    coarse_cells = PATCH * PATCH

    n_idx = jnp.arange(fine_cells, dtype=jnp.int32)
    fi = n_idx // FINE
    fj = n_idx % FINE
    coarse_of = (fi // RATIO) * PATCH + (fj // RATIO)
    m_idx = jnp.arange(coarse_cells, dtype=jnp.int32)
    spread = (m_idx[:, None] == coarse_of[None, :]).astype(jnp.float32)
    blocks = nest_block_state[0, 0].reshape(slots * 3 * level_stack, fine_cells)
    pad_lo = jnp.concatenate([blocks[:, :FINE], blocks[:, :-FINE]], axis=1)
    pad_hi = jnp.concatenate([blocks[:, FINE:], blocks[:, -FINE:]], axis=1)
    left = jnp.concatenate([blocks[:, :1], blocks[:, :-1]], axis=1)
    right = jnp.concatenate([blocks[:, 1:], blocks[:, -1:]], axis=1)
    left = jnp.where((fj == 0)[None, :], blocks, left)
    right = jnp.where((fj == FINE - 1)[None, :], blocks, right)
    lap = pad_hi + pad_lo + right + left - 4.0 * blocks
    smoothed = blocks + KAPPA * lap
    smooth_means = (jnp.dot(smoothed, spread.T, precision=HI) / float(RATIO * RATIO)).reshape(
        slots, cells
    )

    mine = parent_tile_index.reshape(slots)
    spots = parent_spot_index.reshape(slots)
    local = jnp.arange(slots, dtype=jnp.int32)
    rank = jnp.sum(
        ((mine[:, None] == mine[None, :]) & (local[None, :] < local[:, None])).astype(jnp.int32),
        axis=1,
    )
    slot_of = mine * capacity + rank
    slot_hit = (jnp.arange(width, dtype=jnp.int32)[:, None] == slot_of[None, :]).astype(
        jnp.float32
    )
    payload = jnp.concatenate(
        [(spots + 1).astype(jnp.float32)[:, None], smooth_means], axis=1
    )
    outgoing = jnp.dot(slot_hit, payload, precision=HI)
    strips0 = edge_strips((tile[0], tile[1], tile[2]))
    columns0 = column_halos(strips0[2], strips0[3])
    ask_out = jnp.concatenate(
        [
            outgoing.reshape(devices_y, 1, capacity * (cells + 1)),
            columns0.reshape(devices_y, 1, -1),
        ],
        axis=2,
    )
    ask_in = lax.all_to_all(ask_out, "gy", split_axis=0, concat_axis=0, tiled=True)
    asked_payload = ask_in[:, 0, : capacity * (cells + 1)].reshape(width, cells + 1)
    got0 = ask_in[:, 0, capacity * (cells + 1) :].reshape(columns0.shape)
    asked = asked_payload[:, 0].astype(jnp.int32) - 1
    asked_means = asked_payload[:, 1:].reshape(width, 3, level_stack, PATCH, PATCH)

    valid = asked >= 0
    row0 = (asked // qy) * PATCH
    col0 = (asked % qy) * PATCH
    offs = jnp.arange(PATCH, dtype=jnp.int32)
    rows_at = jnp.arange(side_x, dtype=jnp.int32)
    cols_at = jnp.arange(side_y, dtype=jnp.int32)
    row_sel = (
        (rows_at[None, None, :] == (row0[:, None, None] + offs[None, :, None]))
        & valid[:, None, None]
    ).astype(jnp.float32)
    col_sel = (cols_at[None, None, :] == (col0[:, None, None] + offs[None, :, None])).astype(
        jnp.float32
    )
    picked_rows = jnp.einsum("kar,flrc->kflac", row_sel, tile, precision=HI)
    picked = jnp.einsum("kflac,kbc->kflab", picked_rows, col_sel, precision=HI)
    codes = edge_rotation[0]
    flags = [
        my_column == 0,
        my_column == lax.axis_size("gx") - 1,
        my_row == 0,
        my_row == devices_y - 1,
    ]
    turns = edge_turns(codes)
    cell_coriolis = coriolis[0][None]
    south0, north0 = received_columns(got0)
    fields = substep(
        (tile[0], tile[1], tile[2]), strips0, south0, north0, cell_coriolis, turns, flags
    )
    strips1 = edge_strips(fields)
    columns1 = column_halos(strips1[2], strips1[3])
    answer_out = jnp.concatenate(
        [picked.reshape(devices_y, 1, capacity * cells), columns1.reshape(devices_y, 1, -1)],
        axis=2,
    )
    answer_in = lax.all_to_all(answer_out, "gy", split_axis=0, concat_axis=0, tiled=True)
    incoming = answer_in[:, 0, : capacity * cells].reshape(width, cells)
    got1 = answer_in[:, 0, capacity * cells :].reshape(columns1.shape)
    south1, north1 = received_columns(got1)
    fields = substep(fields, strips1, south1, north1, cell_coriolis, turns, flags)

    parent = jnp.dot(slot_hit.T, incoming, precision=HI)
    coarse = parent.reshape(slots * 3 * level_stack, coarse_cells)
    upsampled = jnp.dot(coarse, spread, precision=HI)
    blended = smoothed + ALPHA * (upsampled - smoothed)

    block_mean = asked_means + ALPHA * (picked - asked_means)
    spread_cols = jnp.einsum("kflab,kbc->kflac", block_mean, col_sel, precision=HI)
    dense = jnp.einsum("kar,kflac->flrc", row_sel, spread_cols, precision=HI)
    row_mask = jnp.sum(row_sel, axis=1)
    col_mask = jnp.sum(col_sel, axis=1)
    count = jnp.dot(row_mask.T, col_mask, precision=HI)
    dense, count = lax.optimization_barrier((dense, count))
    after = jnp.stack(fields, axis=0)
    final_result = after + BETA * (dense - count[None, None] * after)
    return (final_result[None], blended.reshape(1, 1, slots, 3, level_stack, fine_cells))


def solution(mesh):
    in_specs = (
        P("panel", None, None, "gx", "gy"),
        P("panel", "gx", "gy"),
        P("panel", None),
        P("panel", "gx", "gy", None, None, None),
        P("panel", "gx", "gy", None),
        P("panel", "gx", "gy"),
    )
    out_specs = (P("panel", None, None, "gx", "gy"), P("panel", "gx", "gy", None, None, None))
    return jax.shard_map(step, mesh=mesh, in_specs=in_specs, out_specs=out_specs, check_vma=False)
```

```python
import jax
import jax.numpy as jnp
from jax import lax
from jax.sharding import PartitionSpec as P

PATCH = 8
RATIO = 3
FINE = 24


DT_STEP = 0.25
GRAVITY = 1.0
DAMPING = 0.5
DEPTH = 1.0
KAPPA = 0.2
ALPHA = 0.5
BETA = 0.5

HI = lax.Precision.HIGHEST


def shift_pairs(count, step):
    return [(i, i + step) for i in range(count) if 0 <= i + step < count]


def centre(field):
    return field[..., 1:-1, 1:-1]


def along_x(field):
    return 0.5 * (field[..., 2:, 1:-1] - field[..., :-2, 1:-1])


def along_y(field):
    return 0.5 * (field[..., 1:-1, 2:] - field[..., 1:-1, :-2])


def laplacian(field):
    return (
        field[..., 2:, 1:-1]
        + field[..., :-2, 1:-1]
        + field[..., 1:-1, 2:]
        + field[..., 1:-1, :-2]
        - 4.0 * centre(field)
    )


def advance(height, east, north, coriolis):
    absolute = coriolis + along_x(north) - along_y(east)
    depth = DEPTH + height
    divergence = along_x(depth * east) + along_y(depth * north)
    new_height = centre(height) - DT_STEP * divergence
    new_east = centre(east) + DT_STEP * (
        absolute * centre(north) - GRAVITY * along_x(height) + DAMPING * laplacian(east)
    )
    new_north = centre(north) + DT_STEP * (
        -absolute * centre(east) - GRAVITY * along_y(height) + DAMPING * laplacian(north)
    )
    return (new_height, new_east, new_north)


def padded_field(field, west, east, south, north):
    rows = jnp.concatenate([west[:, None, :], field, east[:, None, :]], axis=1)
    zero = jnp.zeros_like(south[:, :1])
    low = jnp.concatenate([zero, south, zero], axis=1)[:, :, None]
    high = jnp.concatenate([zero, north, zero], axis=1)[:, :, None]
    return jnp.concatenate([low, rows, high], axis=2)


def edge_turns(codes):
    along = (codes == 0).astype(jnp.float32) - (codes == 2).astype(jnp.float32)
    across = (codes == 3).astype(jnp.float32) - (codes == 1).astype(jnp.float32)
    one = jnp.ones_like(along)
    zero = jnp.zeros_like(along)
    return jnp.stack(
        [
            jnp.stack([one, zero, zero], axis=1),
            jnp.stack([zero, along, across], axis=1),
            jnp.stack([zero, -across, along], axis=1),
        ],
        axis=1,
    )


def edge_strips(fields):
    first_rows = jnp.stack([f[:, 0, :] for f in fields], axis=0)
    last_rows = jnp.stack([f[:, -1, :] for f in fields], axis=0)
    first_cols = jnp.stack([f[:, :, 0] for f in fields], axis=0)
    last_cols = jnp.stack([f[:, :, -1] for f in fields], axis=0)
    return first_rows, last_rows, first_cols, last_cols


def column_halos(first_cols, last_cols):
    count = lax.axis_size("gy")
    here = lax.axis_index("gy")
    target = jnp.arange(count, dtype=jnp.int32)
    to_next = (target == here + 1)[:, None, None, None]
    to_prev = (target == here - 1)[:, None, None, None]
    return jnp.where(to_next, last_cols[None], jnp.where(to_prev, first_cols[None], 0.0))


def received_columns(got):
    count = lax.axis_size("gy")
    here = lax.axis_index("gy")
    south = lax.dynamic_index_in_dim(got, jnp.maximum(here - 1, 0), axis=0, keepdims=False)
    north = lax.dynamic_index_in_dim(got, jnp.minimum(here + 1, count - 1), axis=0, keepdims=False)
    return south, north


def substep(fields, strips, from_south, from_north, coriolis, turns, flags):
    nx = lax.axis_size("gx")
    first_rows, last_rows, first_cols, last_cols = strips
    edges = jnp.stack([first_rows, last_rows, first_cols, last_cols], axis=0)
    partner = lax.ppermute(edges, "panel", [(0, 1), (1, 0)])
    from_west = lax.ppermute(last_rows, "gx", shift_pairs(nx, 1))
    from_east = lax.ppermute(first_rows, "gx", shift_pairs(nx, -1))
    turned = jnp.einsum("sij,sjlc->silc", turns, partner, precision=HI)
    halos = [
        jnp.where(flags[side], turned[side], neighbour)
        for side, neighbour in enumerate((from_west, from_east, from_south, from_north))
    ]
    padded = [padded_field(fields[c], *(h[c] for h in halos)) for c in range(3)]
    return advance(padded[0], padded[1], padded[2], coriolis)


def step(state, coriolis, edge_rotation, nest_block_state, parent_tile_index, parent_spot_index):
    devices_y = lax.axis_size("gy")
    slots = nest_block_state.shape[2]
    capacity = 2
    width = devices_y * capacity
    my_row = lax.axis_index("gy")
    my_column = lax.axis_index("gx")
    tile = state[0]
    level_stack = tile.shape[1]
    side_x = tile.shape[2]
    side_y = tile.shape[3]
    qy = side_y // PATCH
    cells = 3 * level_stack * PATCH * PATCH
    fine_cells = FINE * FINE
    coarse_cells = PATCH * PATCH

    n_idx = jnp.arange(fine_cells, dtype=jnp.int32)
    fi = n_idx // FINE
    fj = n_idx % FINE
    coarse_of = (fi // RATIO) * PATCH + (fj // RATIO)
    m_idx = jnp.arange(coarse_cells, dtype=jnp.int32)
    spread = (m_idx[:, None] == coarse_of[None, :]).astype(jnp.float32)
    blocks = nest_block_state[0, 0].reshape(slots * 3 * level_stack, fine_cells)
    pad_lo = jnp.concatenate([blocks[:, :FINE], blocks[:, :-FINE]], axis=1)
    pad_hi = jnp.concatenate([blocks[:, FINE:], blocks[:, -FINE:]], axis=1)
    left = jnp.concatenate([blocks[:, :1], blocks[:, :-1]], axis=1)
    right = jnp.concatenate([blocks[:, 1:], blocks[:, -1:]], axis=1)
    left = jnp.where((fj == 0)[None, :], blocks, left)
    right = jnp.where((fj == FINE - 1)[None, :], blocks, right)
    lap = pad_hi + pad_lo + right + left - 4.0 * blocks
    smoothed = blocks + KAPPA * lap
    smooth_means = (jnp.dot(smoothed, spread.T, precision=HI) / float(RATIO * RATIO)).reshape(
        slots, cells
    )

    mine = parent_tile_index.reshape(slots)
    spots = parent_spot_index.reshape(slots)
    local = jnp.arange(slots, dtype=jnp.int32)
    rank = jnp.sum(
        ((mine[:, None] == mine[None, :]) & (local[None, :] < local[:, None])).astype(jnp.int32),
        axis=1,
    )
    slot_of = mine * capacity + rank
    slot_hit = (jnp.arange(width, dtype=jnp.int32)[:, None] == slot_of[None, :]).astype(
        jnp.float32
    )
    payload = jnp.concatenate(
        [(spots + 1).astype(jnp.float32)[:, None], smooth_means], axis=1
    )
    outgoing = jnp.dot(slot_hit, payload, precision=HI)
    strips0 = edge_strips((tile[0], tile[1], tile[2]))
    columns0 = column_halos(strips0[2], strips0[3])
    ask_out = jnp.concatenate(
        [
            outgoing.reshape(devices_y, 1, capacity * (cells + 1)),
            columns0.reshape(devices_y, 1, -1),
        ],
        axis=2,
    )
    lanes = -ask_out.shape[2] % 128
    ask_out = jnp.pad(ask_out, ((0, 0), (0, 0), (0, lanes)))
    ask_in = lax.all_to_all(ask_out, "gy", split_axis=0, concat_axis=0, tiled=True)
    asked_payload = ask_in[:, 0, : capacity * (cells + 1)].reshape(width, cells + 1)
    got0 = ask_in[:, 0, capacity * (cells + 1) : capacity * (cells + 1) + columns0[0].size].reshape(
        columns0.shape
    )
    asked = asked_payload[:, 0].astype(jnp.int32) - 1
    asked_means = asked_payload[:, 1:].reshape(width, 3, level_stack, PATCH, PATCH)

    valid = asked >= 0
    row0 = (asked // qy) * PATCH
    col0 = (asked % qy) * PATCH
    offs = jnp.arange(PATCH, dtype=jnp.int32)
    rows_at = jnp.arange(side_x, dtype=jnp.int32)
    cols_at = jnp.arange(side_y, dtype=jnp.int32)
    row_sel = (
        (rows_at[None, None, :] == (row0[:, None, None] + offs[None, :, None]))
        & valid[:, None, None]
    ).astype(jnp.float32)
    col_sel = (cols_at[None, None, :] == (col0[:, None, None] + offs[None, :, None])).astype(
        jnp.float32
    )
    picked_rows = jnp.einsum("kar,flrc->kflac", row_sel, tile, precision=HI)
    picked = jnp.einsum("kflac,kbc->kflab", picked_rows, col_sel, precision=HI)
    codes = edge_rotation[0]
    flags = [
        my_column == 0,
        my_column == lax.axis_size("gx") - 1,
        my_row == 0,
        my_row == devices_y - 1,
    ]
    turns = edge_turns(codes)
    cell_coriolis = coriolis[0][None]
    south0, north0 = received_columns(got0)
    fields = substep(
        (tile[0], tile[1], tile[2]), strips0, south0, north0, cell_coriolis, turns, flags
    )
    strips1 = edge_strips(fields)
    columns1 = column_halos(strips1[2], strips1[3])
    answer_out = jnp.concatenate(
        [picked.reshape(devices_y, 1, capacity * cells), columns1.reshape(devices_y, 1, -1)],
        axis=2,
    )
    answer_in = lax.all_to_all(answer_out, "gy", split_axis=0, concat_axis=0, tiled=True)
    incoming = answer_in[:, 0, : capacity * cells].reshape(width, cells)
    got1 = answer_in[:, 0, capacity * cells :].reshape(columns1.shape)
    south1, north1 = received_columns(got1)
    fields = substep(fields, strips1, south1, north1, cell_coriolis, turns, flags)

    parent = jnp.dot(slot_hit.T, incoming, precision=HI)
    coarse = parent.reshape(slots * 3 * level_stack, coarse_cells)
    upsampled = jnp.dot(coarse, spread, precision=HI)
    blended = smoothed + ALPHA * (upsampled - smoothed)

    block_mean = asked_means + ALPHA * (picked - asked_means)
    spread_cols = jnp.einsum("kflab,kbc->kflac", block_mean, col_sel, precision=HI)
    dense = jnp.einsum("kar,kflac->flrc", row_sel, spread_cols, precision=HI)
    row_mask = jnp.sum(row_sel, axis=1)
    col_mask = jnp.sum(col_sel, axis=1)
    count = jnp.dot(row_mask.T, col_mask, precision=HI)
    dense, count = lax.optimization_barrier((dense, count))
    after = jnp.stack(fields, axis=0)
    final_result = after + BETA * (dense - count[None, None] * after)
    return (final_result[None], blended.reshape(1, 1, slots, 3, level_stack, fine_cells))


def solution(mesh):
    in_specs = (
        P("panel", None, None, "gx", "gy"),
        P("panel", "gx", "gy"),
        P("panel", None),
        P("panel", "gx", "gy", None, None, None),
        P("panel", "gx", "gy", None),
        P("panel", "gx", "gy"),
    )
    out_specs = (P("panel", None, None, "gx", "gy"), P("panel", "gx", "gy", None, None, None))
    return jax.shard_map(step, mesh=mesh, in_specs=in_specs, out_specs=out_specs, check_vma=False)
```
